1024 devices in a mesh: seq: 256 (over z, x, core), head: 4 (over y).
Axes of the slice: x: 4, y: 4, z: 32, core: 2. Of those that a mesh axis runs over, the one named last changes fastest.
Arguments:
- grad_out: bfloat16 [32768, 4096], P('seq', 'head'), may hold values from -48 to 48
- out_weight: bfloat16 [2048, 4096], P('head'), may hold values from -0.09375 to 0.09375
- queries: bfloat16 [32768, 2048], P('seq', 'head'), may hold values from -48 to 48
- keys: bfloat16 [32768, 2048], P('seq', 'head'), may hold values from -6 to 6
- values: bfloat16 [32768, 2048], P('seq', 'head'), may hold values from -6 to 6
- offsets: int32 [2, 16], P(None, 'head'), may hold values from 0 to 15, as said below
Outputs:
- query_grad: bfloat16 [32768, 2048], P('seq', 'head')
- key_grad: bfloat16 [32768, 2048], P('seq', 'head')
- value_grad: bfloat16 [32768, 2048], P('seq', 'head')
The draws below stay inside these ranges and needn't reach their ends.
Inputs may be any that keep to these rules, and one draw needn't show every extreme that they name: offsets[b, h] is below 4^(b+1).
All inputs are finite; a program needn't handle non-finite values.
Results may differ from the reference program's by a relative error of at most 0.0095.
Values may be sent and summed in bfloat16 or wider, within the bound.
No kernel may reach another device: no remote copies, remote signals or barrier semaphores. Data moves between devices by JAX's collectives and lax.ppermute only.
A program may use at most 32 MiB of HBM per device.

```python
import jax
import jax.numpy as jnp
from jax import lax

D = 4096
HEAD_TOTAL = 16
HDIM = 128
TOK_DEV = 128
TOKENS = 32768
DILATED_BRANCHES = 2
N_SEQ = 256


def paired_rows(key):
    width_all = HEAD_TOTAL * HDIM
    base_key = jax.random.fold_in(key, 101)
    query_key = jax.random.fold_in(key, 102)
    key_rows = jnp.clip(jax.random.normal(base_key, (TOKENS, width_all), jnp.float32), -4.0, 4.0)
    query_rows = jnp.clip(jax.random.normal(query_key, (TOKENS, width_all), jnp.float32), -4.0, 4.0)
    return (query_rows, key_rows)


def draw_queries(key, part):
    query_rows, key_rows = paired_rows(key)
    return query_rows.astype(jnp.bfloat16)


def draw_keys(key, part):
    query_rows, key_rows = paired_rows(key)
    return key_rows.astype(jnp.bfloat16)


def draw_offsets(key, part):
    upper_limits = 4 ** (jnp.arange(DILATED_BRANCHES) + 1)
    sampled_rows = jax.random.randint(jax.random.fold_in(key, 201), (DILATED_BRANCHES, HEAD_TOTAL), 0, upper_limits[:, None])
    highest_head = jax.random.randint(jax.random.fold_in(key, 202), (), 0, HEAD_TOTAL)
    low_head = jax.random.randint(jax.random.fold_in(key, 203), (), 0, HEAD_TOTAL)
    branch_row_block = jnp.arange(DILATED_BRANCHES)[:, None]
    head_columns = jnp.arange(HEAD_TOTAL)[None, :]
    sampled_rows = jnp.where((branch_row_block == 0) & (head_columns == low_head), 0, sampled_rows)
    sampled_rows = jnp.where((branch_row_block == DILATED_BRANCHES - 1) & (head_columns == highest_head), 4 ** DILATED_BRANCHES - 1, sampled_rows)
    return sampled_rows.astype(jnp.int32)


def steps_of(key, shape, shards, low, largest):
    factor_of, own = 1.0, jax.random.fold_in(key, 6)
    for axis_at, shards_of in shards:
        draws = jnp.exp(jax.random.uniform(jax.random.fold_in(own, axis_at), (shards_of,), jnp.float32, low / len(shards), largest / len(shards)))
        factor_of = factor_of * jnp.repeat(draws, shape[axis_at] // shards_of).reshape([-1 if axis == axis_at else 1 for axis in range(len(shape))])
    return factor_of


def normal_values(rng, dims, width, most, shards=(), held_as=jnp.bfloat16):
    level = steps_of(rng, dims, shards, -0.22, 0.18) if shards else 1.0
    values = jax.random.normal(rng, dims, jnp.float32) * width * level
    return jnp.minimum(jnp.maximum(values, -most), most).astype(held_as)


def setup_inputs(seed: int = 0) -> dict:
    seeds = jax.random.split(jax.random.key(seed), 7)
    return {
        "grad_out": normal_values(seeds[0], (TOKENS, D), 8.0, 48.0, ((0, 256), (1, 4))),
        "out_weight": normal_values(seeds[1], (HEAD_TOTAL * HDIM, D), D ** -0.5, 0.09375, ((0, 4),)),
        "queries": draw_queries(jax.random.fold_in(seeds[6], 71), 0),
        "keys": draw_keys(jax.random.fold_in(seeds[6], 71), 0),
        "values": normal_values(seeds[4], (TOKENS, HEAD_TOTAL * HDIM), 1.0, 6.0, ((0, 256), (1, 4))),
        "offsets": draw_offsets(jax.random.fold_in(seeds[6], 71), 0),
    }


def pick_rows(block, chosen):
    dilation = chosen.shape[0]
    shaped = block.reshape((block.shape[0] // dilation, dilation) + block.shape[1:])
    widened = chosen.reshape((1,) + chosen.shape + (1,) * (block.ndim - 2))
    return jnp.sum(jnp.where(widened, shaped, jnp.zeros((), block.dtype)), axis=1).astype(block.dtype)


def spread_rows(picked, chosen, filler):
    dilation = chosen.shape[0]
    widened = chosen.reshape((1,) + chosen.shape + (1,) * (picked.ndim - 2))
    placed = jnp.where(widened, picked[:, None], jnp.asarray(filler, picked.dtype))
    return placed.reshape((picked.shape[0] * dilation,) + picked.shape[1:])


def block_scores(query_rows, key_rows, key_live):
    scores = jnp.einsum("qhd,khd->hqk", query_rows.astype(jnp.float32), key_rows.astype(jnp.float32)) * (HDIM ** -0.5)
    return jnp.where(key_live[None, None, :], scores, -jnp.inf)


def block_stats(packed):
    query_rows, key_rows, key_live = packed
    scores = block_scores(query_rows, key_rows, key_live)
    peak = jnp.max(scores, axis=2)
    total = jnp.sum(jnp.exp(scores - peak[:, :, None]), axis=2)
    return peak.T, total.T


def block_output(packed):
    query_rows, key_rows, value_rows, key_live, log_total = packed
    probs = jnp.exp(block_scores(query_rows, key_rows, key_live) - log_total.T[:, :, None])
    weights = probs.astype(jnp.bfloat16)
    return jnp.einsum("hqk,khd->qhd", weights.astype(jnp.float32), value_rows.astype(jnp.float32))


def block_grads(packed):
    query_rows, key_rows, value_rows, out_grad, key_live, log_total, inner = packed
    probs = jnp.exp(block_scores(query_rows, key_rows, key_live) - log_total.T[:, :, None])
    weights = probs.astype(jnp.bfloat16).astype(jnp.float32)
    flow = jnp.einsum("qhd,khd->hqk", out_grad.astype(jnp.float32), value_rows.astype(jnp.float32))
    slope = (probs * (flow - inner.T[:, :, None])).astype(jnp.bfloat16).astype(jnp.float32)
    scale = HDIM ** -0.5
    query_part = jnp.einsum("hqk,khd->qhd", slope, key_rows.astype(jnp.float32)) * scale
    key_part = jnp.einsum("hqk,qhd->khd", slope, query_rows.astype(jnp.float32)) * scale
    value_part = jnp.einsum("hqk,qhd->khd", weights, out_grad.astype(jnp.float32))
    return query_part, key_part, value_part


def reference(grad_out, out_weight, queries, keys, values, offsets):
    row_count = TOK_DEV
    shard_count = N_SEQ
    total_rows = TOKENS
    segment_rows = 2 * row_count
    view = (total_rows, HEAD_TOTAL, HDIM)
    attn_grad = jnp.dot(grad_out, out_weight.T, preferred_element_type=jnp.float32).astype(jnp.bfloat16)
    query_all = queries.reshape(view)
    key_all = keys.reshape(view)
    value_all = values.reshape(view)
    grad_all = attn_grad.reshape(view)

    def blocked(array, group_rows):
        return array.reshape((array.shape[0] // group_rows, group_rows) + array.shape[1:])

    key_blocks = blocked(key_all, row_count)
    value_blocks = blocked(value_all, row_count)
    near_keys = jnp.concatenate([jnp.concatenate([jnp.zeros_like(key_blocks[:1]), key_blocks[:-1]], 0), key_blocks], 1)
    near_values = jnp.concatenate([jnp.concatenate([jnp.zeros_like(value_blocks[:1]), value_blocks[:-1]], 0), value_blocks], 1)
    first_live = jnp.arange(shard_count) > 0
    near_live = jnp.concatenate([jnp.broadcast_to(first_live[:, None], (shard_count, row_count)), jnp.ones((shard_count, row_count), jnp.bool_)], 1)
    near_query = blocked(query_all, row_count)
    near_grad = blocked(grad_all, row_count)

    branches = []
    for branch_index in range(1, DILATED_BRANCHES + 1):
        dilation = 4 ** branch_index
        chosen = jnp.arange(dilation)[:, None] == offsets[branch_index - 1][None, :]
        seg_query = blocked(pick_rows(query_all, chosen), segment_rows)
        seg_key = blocked(pick_rows(key_all, chosen), segment_rows)
        seg_value = blocked(pick_rows(value_all, chosen), segment_rows)
        seg_grad = blocked(pick_rows(grad_all, chosen), segment_rows)
        seg_live = jnp.ones(seg_query.shape[:2], jnp.bool_)
        branches.append((chosen, seg_query, seg_key, seg_value, seg_grad, seg_live))

    near_peak, near_total = lax.map(block_stats, (near_query, near_keys, near_live))
    near_peak = near_peak.reshape(total_rows, HEAD_TOTAL)
    near_total = near_total.reshape(total_rows, HEAD_TOTAL)
    peak = near_peak
    branch_stats = []
    for chosen, seg_query, seg_key, seg_value, seg_grad, seg_live in branches:
        seg_peak, seg_total = lax.map(block_stats, (seg_query, seg_key, seg_live))
        seg_peak = seg_peak.reshape(-1, HEAD_TOTAL)
        seg_total = seg_total.reshape(-1, HEAD_TOTAL)
        branch_stats.append((seg_peak, seg_total))
        peak = jnp.maximum(peak, spread_rows(seg_peak, chosen, -jnp.inf))
    total = near_total * jnp.exp(near_peak - peak)
    for index_branch in range(len(branches)):
        chosen = branches[index_branch][0]
        seg_peak, seg_total = branch_stats[index_branch]
        total = total + spread_rows(seg_total * jnp.exp(seg_peak - pick_rows(peak, chosen)), chosen, 0.0)
    log_total = peak + jnp.log(total)

    output = lax.map(block_output, (near_query, near_keys, near_values, near_live, blocked(log_total, row_count))).reshape(view)
    for chosen, seg_query, seg_key, seg_value, seg_grad, seg_live in branches:
        seg_log = blocked(pick_rows(log_total, chosen), segment_rows)
        seg_out = lax.map(block_output, (seg_query, seg_key, seg_value, seg_live, seg_log))
        output = output + spread_rows(seg_out.reshape(-1, HEAD_TOTAL, HDIM), chosen, 0.0)
    inner = jnp.sum(grad_all.astype(jnp.float32) * output, axis=2)

    near_qgrad, near_kgrad, near_vgrad = lax.map(block_grads, (near_query, near_keys, near_values, near_grad, near_live, blocked(log_total, row_count), blocked(inner, row_count)))
    query_grad = near_qgrad.reshape(view)
    key_grad = (near_kgrad[:, row_count:] + jnp.concatenate([near_kgrad[1:, :row_count], jnp.zeros_like(near_kgrad[:1, :row_count])], 0)).reshape(view)
    value_grad = (near_vgrad[:, row_count:] + jnp.concatenate([near_vgrad[1:, :row_count], jnp.zeros_like(near_vgrad[:1, :row_count])], 0)).reshape(view)
    for chosen, seg_query, seg_key, seg_value, seg_grad, seg_live in branches:
        seg_log = blocked(pick_rows(log_total, chosen), segment_rows)
        seg_inner = blocked(pick_rows(inner, chosen), segment_rows)
        part_query, part_key, part_value = lax.map(block_grads, (seg_query, seg_key, seg_value, seg_grad, seg_live, seg_log, seg_inner))
        query_grad = query_grad + spread_rows(part_query.reshape(-1, HEAD_TOTAL, HDIM), chosen, 0.0)
        key_grad = key_grad + spread_rows(part_key.reshape(-1, HEAD_TOTAL, HDIM), chosen, 0.0)
        value_grad = value_grad + spread_rows(part_value.reshape(-1, HEAD_TOTAL, HDIM), chosen, 0.0)
    flat = (total_rows, HEAD_TOTAL * HDIM)
    return (query_grad.astype(jnp.bfloat16).reshape(flat), key_grad.astype(jnp.bfloat16).reshape(flat), value_grad.astype(jnp.bfloat16).reshape(flat))
```

```python
import jax
import jax.numpy as jnp
from jax import lax
from jax.sharding import PartitionSpec as P

HDIM = 128


def partner(shard, axis, stride):
    return lax.ppermute(shard, axis, [(i, i ^ 1 << stride) for i in range(lax.axis_size(axis))])


def shifted(value, axis, steps):
    count = lax.axis_size(axis)
    initial, last = (max(0, -steps), min(count, count - steps))
    return lax.ppermute(value, axis, [(source, source + steps) for source in range(initial, last)])


def pick_rows(block, chosen):
    dilation = chosen.shape[0]
    head_count = block.shape[0]
    shaped = block.reshape((head_count, block.shape[1] // dilation, dilation) + block.shape[2:])
    widened = chosen.T.reshape((head_count, 1, dilation) + (1,) * (block.ndim - 2))
    return jnp.sum(jnp.where(widened, shaped, jnp.zeros((), block.dtype)), axis=2)


def spread_rows(picked, chosen, filler):
    dilation = chosen.shape[0]
    head_count = picked.shape[0]
    widened = chosen.T.reshape((head_count, 1, dilation) + (1,) * (picked.ndim - 2))
    placed = jnp.where(widened, picked[:, :, None], jnp.asarray(filler, picked.dtype))
    return placed.reshape((head_count, picked.shape[1] * dilation) + picked.shape[2:])


def block_scores(query_rows, key_rows, key_live):
    scores = jnp.einsum(
        "hqd,hkd->hqk", query_rows, key_rows, preferred_element_type=jnp.float32
    ) * HDIM ** (-0.5)
    return jnp.where(key_live[None, None, :], scores, -jnp.inf)


def block_stats(scores):
    peak = jnp.max(scores, axis=2)
    total = jnp.sum(jnp.exp(scores - peak[:, :, None]), axis=2)
    return (peak, total)


def block_output(scores, value_rows, log_total):
    probs = jnp.exp(scores - log_total[:, :, None])
    weights = probs.astype(jnp.bfloat16)
    return jnp.einsum("hqk,hkd->hqd", weights, value_rows, preferred_element_type=jnp.float32)


def block_grads(scores, query_rows, key_rows, value_rows, out_grad, log_total, inner):
    probs = jnp.exp(scores - log_total[:, :, None])
    weights = probs.astype(jnp.bfloat16)
    flow = jnp.einsum("hqd,hkd->hqk", out_grad, value_rows, preferred_element_type=jnp.float32)
    slope = (probs * (flow - inner[:, :, None])).astype(jnp.bfloat16)
    scale = HDIM ** (-0.5)
    query_part = (
        jnp.einsum("hqk,hkd->hqd", slope, key_rows, preferred_element_type=jnp.float32) * scale
    )
    key_part = (
        jnp.einsum("hqk,hqd->hkd", slope, query_rows, preferred_element_type=jnp.float32) * scale
    )
    value_part = jnp.einsum("hqk,hqd->hkd", weights, out_grad, preferred_element_type=jnp.float32)
    return (query_part, key_part, value_part)


def exchange(arrays, bit_pos):
    sizes = [array.shape[1] for array in arrays]
    packed = jnp.concatenate(arrays, 1)
    arrived = partner(packed, "seq", bit_pos)
    cuts = [sum(sizes[: index + 1]) for index in range(len(sizes) - 1)]
    return jnp.split(arrived, cuts, axis=1)


def collect_all(groups, seq_index):
    steps_total = max(steps for steps, _ in groups)
    groups = [(steps, list(parts)) for steps, parts in groups]
    for bit_pos in range(steps_total):
        active = [index for index, (steps, _) in enumerate(groups) if steps > bit_pos]
        sending = [part for index in active for part in groups[index][1]]
        arrived = exchange(sending, bit_pos)
        upper = seq_index // 2**bit_pos % 2 == 1
        at = 0
        for index in active:
            parts = groups[index][1]
            merged = []
            for own_part in parts:
                far_part = arrived[at]
                at += 1
                merged.append(
                    jnp.where(
                        upper,
                        jnp.concatenate([far_part, own_part], 1),
                        jnp.concatenate([own_part, far_part], 1),
                    )
                )
            groups[index] = (groups[index][0], merged)
    return [parts for _, parts in groups]


def reduce_all(groups, seq_index):
    steps_total = max(steps for steps, _ in groups)
    groups = [(steps, list(parts)) for steps, parts in groups]
    for bit_pos in reversed(range(steps_total)):
        active = [index for index, (steps, _) in enumerate(groups) if steps > bit_pos]
        upper = seq_index // 2**bit_pos % 2 == 1
        sending = []
        keeping = []
        for index in active:
            for whole_part in groups[index][1]:
                half_rows = whole_part.shape[1] // 2
                sending.append(
                    jnp.where(upper, whole_part[:, :half_rows], whole_part[:, half_rows:])
                )
                keeping.append(
                    jnp.where(upper, whole_part[:, half_rows:], whole_part[:, :half_rows])
                )
        arrived = exchange(sending, bit_pos)
        at = 0
        for index in active:
            count = len(groups[index][1])
            groups[index] = (
                groups[index][0],
                [kept + came for kept, came in zip(keeping[at : at + count], arrived[at : at + count])],
            )
            at += count
    return [parts for _, parts in groups]


def ring_gather(block, axis):
    count = lax.axis_size(axis)
    own = lax.axis_index(axis)
    pieces = [block] + [
        lax.ppermute(block, axis, [(source, (source + step) % count) for source in range(count)])
        for step in range(1, count)
    ]
    stacked = jnp.stack(pieces)
    ordered = jnp.take(stacked, (own - jnp.arange(count)) % count, axis=0)
    return ordered.transpose(1, 0, 2).reshape(block.shape[0], count * block.shape[1])


def per_device(grad_out, out_weight, queries, keys, values, offsets):
    row_count = queries.shape[0]
    head_count = queries.shape[1] // HDIM
    branch_count = offsets.shape[0]
    view = (row_count, head_count, HDIM)

    def to_heads(flat_rows):
        return flat_rows.reshape(view).transpose(1, 0, 2)

    attn_flat = lax.dot_general(
        ring_gather(grad_out, "head"),
        out_weight,
        (((1,), (1,)), ((), ())),
        preferred_element_type=jnp.float32,
    )
    attn_grad = to_heads(attn_flat.astype(jnp.bfloat16))

    query_local = to_heads(queries)
    key_local = to_heads(keys)
    value_local = to_heads(values)
    seq_index = lax.axis_index("seq")
    prior_rows = shifted(jnp.concatenate([keys, values], 1), "seq", 1)
    prior_keys, prior_values = jnp.split(prior_rows, 2, axis=1)
    near_keys = jnp.concatenate([to_heads(prior_keys), key_local], 1)
    near_values = jnp.concatenate([to_heads(prior_values), value_local], 1)
    near_live = jnp.concatenate(
        [jnp.full((row_count,), seq_index > 0), jnp.ones((row_count,), jnp.bool_)]
    )
    picked_all = []
    for branch_index in range(1, branch_count + 1):
        dilation = 4**branch_index
        chosen = jnp.arange(dilation)[:, None] == offsets[branch_index - 1][None, :]
        picked_all.append(
            (
                chosen,
                pick_rows(query_local, chosen),
                pick_rows(key_local, chosen),
                pick_rows(value_local, chosen),
                pick_rows(attn_grad, chosen),
            )
        )
    gathered = collect_all(
        [(2 * index + 1, (entry[2], entry[3])) for index, entry in enumerate(picked_all, 1)],
        seq_index,
    )
    branches = []
    for branch_index in range(1, branch_count + 1):
        chosen, picked_query, picked_key, picked_value, picked_grad = picked_all[branch_index - 1]
        segment_keys, segment_values = gathered[branch_index - 1]
        segment_live = jnp.ones((segment_keys.shape[1],), jnp.bool_)
        seg_scores = block_scores(picked_query, segment_keys, segment_live)
        branches.append(
            (
                branch_index,
                chosen,
                picked_query,
                picked_key,
                picked_value,
                picked_grad,
                segment_keys,
                segment_values,
                seg_scores,
            )
        )
    near_scores = block_scores(query_local, near_keys, near_live)
    near_peak, near_total = block_stats(near_scores)
    peak = near_peak
    branch_stats = []
    for branch_entry in branches:
        chosen = branch_entry[1]
        seg_peak, seg_total = block_stats(branch_entry[8])
        branch_stats.append((seg_peak, seg_total))
        peak = jnp.maximum(peak, spread_rows(seg_peak, chosen, -jnp.inf))
    total = near_total * jnp.exp(near_peak - peak)
    for index_branch in range(len(branches)):
        chosen = branches[index_branch][1]
        seg_peak, seg_total = branch_stats[index_branch]
        total = total + spread_rows(
            seg_total * jnp.exp(seg_peak - pick_rows(peak, chosen)), chosen, 0.0
        )
    log_total = peak + jnp.log(total)
    output = block_output(near_scores, near_values, log_total)
    for (
        branch_index,
        chosen,
        picked_query,
        picked_key,
        picked_value,
        picked_grad,
        segment_keys,
        segment_values,
        seg_scores,
    ) in branches:
        seg_log = pick_rows(log_total, chosen)
        output = output + spread_rows(
            block_output(seg_scores, segment_values, seg_log), chosen, 0.0
        )
    inner = jnp.sum(attn_grad.astype(jnp.float32) * output, axis=2)
    near_qgrad, near_kgrad, near_vgrad = block_grads(
        near_scores, query_local, near_keys, near_values, attn_grad, log_total, inner
    )
    back_rows = shifted(
        jnp.concatenate([near_kgrad[:, :row_count], near_vgrad[:, :row_count]], 1), "seq", -1
    )
    back_keys, back_values = jnp.split(back_rows, 2, axis=1)
    query_grad = near_qgrad
    key_grad = near_kgrad[:, row_count:] + back_keys
    value_grad = near_vgrad[:, row_count:] + back_values
    segment_grads = []
    for (
        branch_index,
        chosen,
        picked_query,
        picked_key,
        picked_value,
        picked_grad,
        segment_keys,
        segment_values,
        seg_scores,
    ) in branches:
        seg_log = pick_rows(log_total, chosen)
        seg_inner = pick_rows(inner, chosen)
        part_query, segment_kgrad, segment_vgrad = block_grads(
            seg_scores, picked_query, segment_keys, segment_values, picked_grad, seg_log, seg_inner
        )
        query_grad = query_grad + spread_rows(part_query, chosen, 0.0)
        segment_grads.append((2 * branch_index + 1, (segment_kgrad, segment_vgrad)))
    owned = reduce_all(segment_grads, seq_index)
    for branch_entry, (own_kgrad, own_vgrad) in zip(branches, owned):
        chosen = branch_entry[1]
        key_grad = key_grad + spread_rows(own_kgrad, chosen, 0.0)
        value_grad = value_grad + spread_rows(own_vgrad, chosen, 0.0)
    flat = (row_count, head_count * HDIM)

    def to_rows(head_major):
        return head_major.astype(jnp.bfloat16).transpose(1, 0, 2).reshape(flat)

    return (to_rows(query_grad), to_rows(key_grad), to_rows(value_grad))


def solution(mesh):
    return jax.shard_map(
        per_device,
        mesh=mesh,
        in_specs=(
            P("seq", "head"),
            P("head", None),
            P("seq", "head"),
            P("seq", "head"),
            P("seq", "head"),
            P(None, "head"),
        ),
        out_specs=(P("seq", "head"), P("seq", "head"), P("seq", "head")),
        check_vma=False,
    )
```

```python
import jax
import jax.numpy as jnp
from jax import lax
from jax.sharding import PartitionSpec as P

HDIM = 128


def partner(shard, axis, stride):
    return lax.ppermute(shard, axis, [(i, i ^ 1 << stride) for i in range(lax.axis_size(axis))])


def shifted(value, axis, steps):
    count = lax.axis_size(axis)
    initial, last = (max(0, -steps), min(count, count - steps))
    return lax.ppermute(value, axis, [(source, source + steps) for source in range(initial, last)])


def pick_rows(block, chosen):
    dilation = chosen.shape[0]
    head_count = block.shape[0]
    shaped = block.reshape((head_count, block.shape[1] // dilation, dilation) + block.shape[2:])
    widened = chosen.T.reshape((head_count, 1, dilation) + (1,) * (block.ndim - 2))
    return jnp.sum(jnp.where(widened, shaped, jnp.zeros((), block.dtype)), axis=2)


def spread_rows(picked, chosen, filler):
    dilation = chosen.shape[0]
    head_count = picked.shape[0]
    widened = chosen.T.reshape((head_count, 1, dilation) + (1,) * (picked.ndim - 2))
    placed = jnp.where(widened, picked[:, :, None], jnp.asarray(filler, picked.dtype))
    return placed.reshape((head_count, picked.shape[1] * dilation) + picked.shape[2:])


def block_scores(query_rows, key_rows, key_live):
    scores = jnp.einsum(
        "hqd,hkd->hqk", query_rows, key_rows, preferred_element_type=jnp.float32
    ) * HDIM ** (-0.5)
    return jnp.where(key_live[None, None, :], scores, -jnp.inf)


def block_stats(scores):
    peak = jnp.max(scores, axis=2)
    total = jnp.sum(jnp.exp(scores - peak[:, :, None]), axis=2)
    return (peak, total)


def block_output(scores, value_rows, log_total):
    probs = jnp.exp(scores - log_total[:, :, None])
    weights = probs.astype(jnp.bfloat16)
    return jnp.einsum("hqk,hkd->hqd", weights, value_rows, preferred_element_type=jnp.float32)


def block_grads(scores, query_rows, key_rows, value_rows, out_grad, log_total, inner):
    probs = jnp.exp(scores - log_total[:, :, None])
    weights = probs.astype(jnp.bfloat16)
    flow = jnp.einsum("hqd,hkd->hqk", out_grad, value_rows, preferred_element_type=jnp.float32)
    slope = (probs * (flow - inner[:, :, None])).astype(jnp.bfloat16)
    scale = HDIM ** (-0.5)
    query_part = (
        jnp.einsum("hqk,hkd->hqd", slope, key_rows, preferred_element_type=jnp.float32) * scale
    )
    key_part = (
        jnp.einsum("hqk,hqd->hkd", slope, query_rows, preferred_element_type=jnp.float32) * scale
    )
    value_part = jnp.einsum("hqk,hqd->hkd", weights, out_grad, preferred_element_type=jnp.float32)
    return (query_part, key_part, value_part)


def exchange(arrays, bit_pos):
    flat = [array.reshape(array.shape[0], -1) for array in arrays]
    sizes = [part.shape[1] for part in flat]
    packed = jnp.concatenate(flat, 1)
    arrived = partner(packed, "seq", bit_pos)
    cuts = [sum(sizes[: index + 1]) for index in range(len(sizes) - 1)]
    return [
        part.reshape(array.shape)
        for part, array in zip(jnp.split(arrived, cuts, axis=1), arrays)
    ]


def collect_all(groups, seq_index):
    steps_total = max(steps for steps, _ in groups)
    groups = [(steps, list(parts)) for steps, parts in groups]
    for bit_pos in range(steps_total):
        active = [index for index, (steps, _) in enumerate(groups) if steps > bit_pos]
        sending = [part for index in active for part in groups[index][1]]
        arrived = exchange(sending, bit_pos)
        upper = seq_index // 2**bit_pos % 2 == 1
        at = 0
        for index in active:
            parts = groups[index][1]
            merged = []
            for own_part in parts:
                far_part = arrived[at]
                at += 1
                merged.append(
                    jnp.where(
                        upper,
                        jnp.concatenate([far_part, own_part], 1),
                        jnp.concatenate([own_part, far_part], 1),
                    )
                )
            groups[index] = (groups[index][0], merged)
    return [parts for _, parts in groups]


def reduce_all(groups, seq_index):
    steps_total = max(steps for steps, _ in groups)
    groups = [(steps, list(parts)) for steps, parts in groups]
    for bit_pos in reversed(range(steps_total)):
        active = [index for index, (steps, _) in enumerate(groups) if steps > bit_pos]
        upper = seq_index // 2**bit_pos % 2 == 1
        sending = []
        keeping = []
        for index in active:
            for whole_part in groups[index][1]:
                half_rows = whole_part.shape[1] // 2
                sending.append(
                    jnp.where(upper, whole_part[:, :half_rows], whole_part[:, half_rows:])
                )
                keeping.append(
                    jnp.where(upper, whole_part[:, half_rows:], whole_part[:, :half_rows])
                )
        arrived = exchange(sending, bit_pos)
        at = 0
        for index in active:
            count = len(groups[index][1])
            groups[index] = (
                groups[index][0],
                [kept + came for kept, came in zip(keeping[at : at + count], arrived[at : at + count])],
            )
            at += count
    return [parts for _, parts in groups]


def ring_gather(block, axis):
    count = lax.axis_size(axis)
    own = lax.axis_index(axis)
    pieces = [block] + [
        lax.ppermute(block, axis, [(source, (source + step) % count) for source in range(count)])
        for step in range(1, count)
    ]
    stacked = jnp.stack(pieces)
    ordered = jnp.take(stacked, (own - jnp.arange(count)) % count, axis=0)
    return ordered.transpose(1, 0, 2).reshape(block.shape[0], count * block.shape[1])


def key_side_grads(key_rows, value_rows, query_rows, out_grad, log_total, inner, live):
    scale = HDIM ** (-0.5)
    scores = jnp.einsum(
        "hkd,hqd->hkq", key_rows, query_rows, preferred_element_type=jnp.float32
    ) * scale
    probs = jnp.exp(scores - log_total[:, None, :])
    probs = jnp.where(live, probs, 0.0)
    weights = probs.astype(jnp.bfloat16)
    flow = jnp.einsum("hkd,hqd->hkq", value_rows, out_grad, preferred_element_type=jnp.float32)
    slope = (probs * (flow - inner[:, None, :])).astype(jnp.bfloat16)
    key_part = (
        jnp.einsum("hkq,hqd->hkd", slope, query_rows, preferred_element_type=jnp.float32) * scale
    )
    value_part = jnp.einsum("hkq,hqd->hkd", weights, out_grad, preferred_element_type=jnp.float32)
    return (key_part, value_part)


def per_device(grad_out, out_weight, queries, keys, values, offsets):
    row_count = queries.shape[0]
    head_count = queries.shape[1] // HDIM
    branch_count = offsets.shape[0]
    view = (row_count, head_count, HDIM)

    def to_heads(flat_rows):
        return flat_rows.reshape(view).transpose(1, 0, 2)

    query_local = to_heads(queries)
    key_local = to_heads(keys)
    value_local = to_heads(values)
    seq_index = lax.axis_index("seq")
    seq_count = lax.axis_size("seq")
    prior_rows = shifted(jnp.concatenate([keys, values], 1), "seq", 1)
    prior_keys, prior_values = jnp.split(prior_rows, 2, axis=1)
    next_queries = to_heads(shifted(queries, "seq", -1))
    near_keys = jnp.concatenate([to_heads(prior_keys), key_local], 1)
    near_values = jnp.concatenate([to_heads(prior_values), value_local], 1)
    near_live = jnp.concatenate(
        [jnp.full((row_count,), seq_index > 0), jnp.ones((row_count,), jnp.bool_)]
    )
    picked_all = []
    for branch_index in range(1, branch_count + 1):
        dilation = 4**branch_index
        chosen = jnp.arange(dilation)[:, None] == offsets[branch_index - 1][None, :]
        picked_all.append(
            (
                chosen,
                pick_rows(query_local, chosen),
                pick_rows(key_local, chosen),
                pick_rows(value_local, chosen),
            )
        )
    gathered = collect_all(
        [(2 * index + 1, (entry[2], entry[3], entry[1])) for index, entry in enumerate(picked_all, 1)],
        seq_index,
    )
    attn_flat = lax.dot_general(
        ring_gather(grad_out, "head"),
        out_weight,
        (((1,), (1,)), ((), ())),
        preferred_element_type=jnp.float32,
    )
    attn_grad = to_heads(attn_flat.astype(jnp.bfloat16))

    near_scores = block_scores(query_local, near_keys, near_live)
    near_peak, near_total = block_stats(near_scores)
    peak = near_peak
    branch_stats = []
    seg_scores_all = []
    for (chosen, picked_query, picked_key, picked_value), (segment_keys, segment_values, _) in zip(
        picked_all, gathered
    ):
        segment_live = jnp.ones((segment_keys.shape[1],), jnp.bool_)
        seg_scores = block_scores(picked_query, segment_keys, segment_live)
        seg_scores_all.append(seg_scores)
        seg_peak, seg_total = block_stats(seg_scores)
        branch_stats.append((seg_peak, seg_total))
        peak = jnp.maximum(peak, spread_rows(seg_peak, chosen, -jnp.inf))
    total = near_total * jnp.exp(near_peak - peak)
    for index_branch in range(branch_count):
        chosen = picked_all[index_branch][0]
        seg_peak, seg_total = branch_stats[index_branch]
        total = total + spread_rows(
            seg_total * jnp.exp(seg_peak - pick_rows(peak, chosen)), chosen, 0.0
        )
    log_total = peak + jnp.log(total)
    output = block_output(near_scores, near_values, log_total)
    for index_branch in range(branch_count):
        chosen = picked_all[index_branch][0]
        segment_values = gathered[index_branch][1]
        seg_log = pick_rows(log_total, chosen)
        output = output + spread_rows(
            block_output(seg_scores_all[index_branch], segment_values, seg_log), chosen, 0.0
        )
    inner = jnp.sum(attn_grad.astype(jnp.float32) * output, axis=2)

    stats_rows = jnp.concatenate(
        [attn_grad.astype(jnp.float32), log_total[:, None, :], inner[:, None, :]], 1
    )
    next_rows = shifted(stats_rows, "seq", -1)
    picked_stats = []
    for index_branch in range(branch_count):
        chosen = picked_all[index_branch][0]
        picked_stats.append(
            (
                2 * index_branch + 3,
                (
                    pick_rows(attn_grad, chosen).astype(jnp.float32),
                    pick_rows(log_total, chosen),
                    pick_rows(inner, chosen),
                ),
            )
        )
    segment_stats = collect_all(picked_stats, seq_index)

    near_qgrad, near_kgrad, near_vgrad = block_grads(
        near_scores, query_local, near_keys, near_values, attn_grad, log_total, inner
    )
    query_grad = near_qgrad
    key_grad = near_kgrad[:, row_count:]
    value_grad = near_vgrad[:, row_count:]
    next_kgrad, next_vgrad = key_side_grads(
        key_local,
        value_local,
        next_queries,
        next_rows[:, :row_count].astype(jnp.bfloat16),
        next_rows[:, row_count],
        next_rows[:, row_count + 1],
        seq_index < seq_count - 1,
    )
    key_grad = key_grad + next_kgrad
    value_grad = value_grad + next_vgrad
    for index_branch in range(branch_count):
        chosen, picked_query, picked_key, picked_value = picked_all[index_branch]
        segment_keys, segment_values, segment_queries = gathered[index_branch]
        seg_grad, seg_log_all, seg_inner_all = segment_stats[index_branch]
        seg_log = pick_rows(log_total, chosen)
        seg_inner = pick_rows(inner, chosen)
        picked_grad = pick_rows(attn_grad, chosen)
        part_query, _, _ = block_grads(
            seg_scores_all[index_branch],
            picked_query,
            segment_keys,
            segment_values,
            picked_grad,
            seg_log,
            seg_inner,
        )
        query_grad = query_grad + spread_rows(part_query, chosen, 0.0)
        own_kgrad, own_vgrad = key_side_grads(
            picked_key,
            picked_value,
            segment_queries,
            seg_grad.astype(jnp.bfloat16),
            seg_log_all,
            seg_inner_all,
            True,
        )
        key_grad = key_grad + spread_rows(own_kgrad, chosen, 0.0)
        value_grad = value_grad + spread_rows(own_vgrad, chosen, 0.0)
    flat = (row_count, head_count * HDIM)

    def to_rows(head_major):
        return head_major.astype(jnp.bfloat16).transpose(1, 0, 2).reshape(flat)

    return (to_rows(query_grad), to_rows(key_grad), to_rows(value_grad))


def solution(mesh):
    return jax.shard_map(
        per_device,
        mesh=mesh,
        in_specs=(
            P("seq", "head"),
            P("head", None),
            P("seq", "head"),
            P("seq", "head"),
            P("seq", "head"),
            P(None, "head"),
        ),
        out_specs=(P("seq", "head"), P("seq", "head"), P("seq", "head")),
        check_vma=False,
    )
```

```python
import jax
import jax.numpy as jnp
from jax import lax
from jax.sharding import PartitionSpec as P

HDIM = 128


def partner(shard, axis, stride):
    return lax.ppermute(shard, axis, [(i, i ^ 1 << stride) for i in range(lax.axis_size(axis))])


def shifted(value, axis, steps):
    count = lax.axis_size(axis)
    initial, last = (max(0, -steps), min(count, count - steps))
    return lax.ppermute(value, axis, [(source, source + steps) for source in range(initial, last)])


def pick_rows(block, chosen):
    dilation = chosen.shape[0]
    head_count = block.shape[0]
    shaped = block.reshape((head_count, block.shape[1] // dilation, dilation) + block.shape[2:])
    widened = chosen.T.reshape((head_count, 1, dilation) + (1,) * (block.ndim - 2))
    return jnp.sum(jnp.where(widened, shaped, jnp.zeros((), block.dtype)), axis=2)


def spread_rows(picked, chosen, filler):
    dilation = chosen.shape[0]
    head_count = picked.shape[0]
    widened = chosen.T.reshape((head_count, 1, dilation) + (1,) * (picked.ndim - 2))
    placed = jnp.where(widened, picked[:, :, None], jnp.asarray(filler, picked.dtype))
    return placed.reshape((head_count, picked.shape[1] * dilation) + picked.shape[2:])


def block_scores(query_rows, key_rows, key_live):
    scores = jnp.einsum(
        "hqd,hkd->hqk", query_rows, key_rows, preferred_element_type=jnp.float32
    ) * HDIM ** (-0.5)
    return jnp.where(key_live[None, None, :], scores, -jnp.inf)


def block_stats(scores):
    peak = jnp.max(scores, axis=2)
    total = jnp.sum(jnp.exp(scores - peak[:, :, None]), axis=2)
    return (peak, total)


def block_output(scores, value_rows, log_total):
    probs = jnp.exp(scores - log_total[:, :, None])
    weights = probs.astype(jnp.bfloat16)
    return jnp.einsum("hqk,hkd->hqd", weights, value_rows, preferred_element_type=jnp.float32)


def block_grads(scores, query_rows, key_rows, value_rows, out_grad, log_total, inner):
    probs = jnp.exp(scores - log_total[:, :, None])
    weights = probs.astype(jnp.bfloat16)
    flow = jnp.einsum("hqd,hkd->hqk", out_grad, value_rows, preferred_element_type=jnp.float32)
    slope = (probs * (flow - inner[:, :, None])).astype(jnp.bfloat16)
    scale = HDIM ** (-0.5)
    query_part = (
        jnp.einsum("hqk,hkd->hqd", slope, key_rows, preferred_element_type=jnp.float32) * scale
    )
    key_part = (
        jnp.einsum("hqk,hqd->hkd", slope, query_rows, preferred_element_type=jnp.float32) * scale
    )
    value_part = jnp.einsum("hqk,hqd->hkd", weights, out_grad, preferred_element_type=jnp.float32)
    return (query_part, key_part, value_part)


def exchange(arrays, bit_pos):
    sizes = [array.shape[1] for array in arrays]
    packed = jnp.concatenate(arrays, 1)
    arrived = partner(packed, "seq", bit_pos)
    cuts = [sum(sizes[: index + 1]) for index in range(len(sizes) - 1)]
    return jnp.split(arrived, cuts, axis=1)


def collect_all(groups, seq_index):
    steps_total = max(steps for steps, _ in groups)
    groups = [(steps, list(parts)) for steps, parts in groups]
    for bit_pos in reversed(range(steps_total)):
        active = [index for index, (steps, _) in enumerate(groups) if steps > bit_pos]
        sending = [part for index in active for part in groups[index][1]]
        arrived = exchange(sending, bit_pos)
        upper = seq_index // 2**bit_pos % 2 == 1
        at = 0
        for index in active:
            parts = groups[index][1]
            merged = []
            for own_part in parts:
                far_part = arrived[at]
                at += 1
                merged.append(
                    jnp.where(
                        upper,
                        jnp.concatenate([far_part, own_part], 1),
                        jnp.concatenate([own_part, far_part], 1),
                    )
                )
            groups[index] = (groups[index][0], merged)
    return [parts for _, parts in groups]


def reduce_all(groups, seq_index):
    steps_total = max(steps for steps, _ in groups)
    groups = [(steps, list(parts)) for steps, parts in groups]
    for bit_pos in range(steps_total):
        active = [index for index, (steps, _) in enumerate(groups) if steps > bit_pos]
        upper = seq_index // 2**bit_pos % 2 == 1
        sending = []
        keeping = []
        for index in active:
            for whole_part in groups[index][1]:
                half_rows = whole_part.shape[1] // 2
                sending.append(
                    jnp.where(upper, whole_part[:, :half_rows], whole_part[:, half_rows:])
                )
                keeping.append(
                    jnp.where(upper, whole_part[:, half_rows:], whole_part[:, :half_rows])
                )
        arrived = exchange(sending, bit_pos)
        at = 0
        for index in active:
            count = len(groups[index][1])
            groups[index] = (
                groups[index][0],
                [kept + came for kept, came in zip(keeping[at : at + count], arrived[at : at + count])],
            )
            at += count
    return [parts for _, parts in groups]


def ring_gather(block, axis):
    count = lax.axis_size(axis)
    own = lax.axis_index(axis)
    pieces = [block] + [
        lax.ppermute(block, axis, [(source, (source + step) % count) for source in range(count)])
        for step in range(1, count)
    ]
    stacked = jnp.stack(pieces)
    ordered = jnp.take(stacked, (own - jnp.arange(count)) % count, axis=0)
    return ordered.transpose(1, 0, 2).reshape(block.shape[0], count * block.shape[1])


def per_device(grad_out, out_weight, queries, keys, values, offsets):
    row_count = queries.shape[0]
    head_count = queries.shape[1] // HDIM
    branch_count = offsets.shape[0]
    view = (row_count, head_count, HDIM)

    def to_heads(flat_rows):
        return flat_rows.reshape(view).transpose(1, 0, 2)

    query_local = to_heads(queries)
    key_local = to_heads(keys)
    value_local = to_heads(values)
    seq_index = lax.axis_index("seq")
    prior_rows = shifted(jnp.concatenate([keys, values], 1), "seq", 1)
    prior_keys, prior_values = jnp.split(prior_rows, 2, axis=1)
    near_keys = jnp.concatenate([to_heads(prior_keys), key_local], 1)
    near_values = jnp.concatenate([to_heads(prior_values), value_local], 1)
    near_live = jnp.concatenate(
        [jnp.full((row_count,), seq_index > 0), jnp.ones((row_count,), jnp.bool_)]
    )
    picked_all = []
    for branch_index in range(1, branch_count + 1):
        dilation = 4**branch_index
        chosen = jnp.arange(dilation)[:, None] == offsets[branch_index - 1][None, :]
        picked_all.append(
            (
                chosen,
                pick_rows(query_local, chosen),
                pick_rows(key_local, chosen),
                pick_rows(value_local, chosen),
            )
        )
    gathered = collect_all(
        [(2 * index + 1, (entry[2], entry[3])) for index, entry in enumerate(picked_all, 1)],
        seq_index,
    )
    gathered_grad, _ = lax.optimization_barrier((ring_gather(grad_out, "head"), gathered[-1][0]))
    attn_flat = lax.dot_general(
        gathered_grad,
        out_weight,
        (((1,), (1,)), ((), ())),
        preferred_element_type=jnp.float32,
    )
    attn_grad = to_heads(attn_flat.astype(jnp.bfloat16))
    branches = []
    for branch_index in range(1, branch_count + 1):
        chosen, picked_query, picked_key, picked_value = picked_all[branch_index - 1]
        picked_grad = pick_rows(attn_grad, chosen)
        segment_keys, segment_values = gathered[branch_index - 1]
        segment_live = jnp.ones((segment_keys.shape[1],), jnp.bool_)
        seg_scores = block_scores(picked_query, segment_keys, segment_live)
        branches.append(
            (
                branch_index,
                chosen,
                picked_query,
                picked_key,
                picked_value,
                picked_grad,
                segment_keys,
                segment_values,
                seg_scores,
            )
        )
    near_scores = block_scores(query_local, near_keys, near_live)
    near_peak, near_total = block_stats(near_scores)
    peak = near_peak
    branch_stats = []
    for branch_entry in branches:
        chosen = branch_entry[1]
        seg_peak, seg_total = block_stats(branch_entry[8])
        branch_stats.append((seg_peak, seg_total))
        peak = jnp.maximum(peak, spread_rows(seg_peak, chosen, -jnp.inf))
    total = near_total * jnp.exp(near_peak - peak)
    for index_branch in range(len(branches)):
        chosen = branches[index_branch][1]
        seg_peak, seg_total = branch_stats[index_branch]
        total = total + spread_rows(
            seg_total * jnp.exp(seg_peak - pick_rows(peak, chosen)), chosen, 0.0
        )
    log_total = peak + jnp.log(total)
    output = block_output(near_scores, near_values, log_total)
    for (
        branch_index,
        chosen,
        picked_query,
        picked_key,
        picked_value,
        picked_grad,
        segment_keys,
        segment_values,
        seg_scores,
    ) in branches:
        seg_log = pick_rows(log_total, chosen)
        output = output + spread_rows(
            block_output(seg_scores, segment_values, seg_log), chosen, 0.0
        )
    inner = jnp.sum(attn_grad.astype(jnp.float32) * output, axis=2)
    near_qgrad, near_kgrad, near_vgrad = block_grads(
        near_scores, query_local, near_keys, near_values, attn_grad, log_total, inner
    )
    back_rows = shifted(
        jnp.concatenate([near_kgrad[:, :row_count], near_vgrad[:, :row_count]], 1), "seq", -1
    )
    back_keys, back_values = jnp.split(back_rows, 2, axis=1)
    query_grad = near_qgrad
    key_grad = near_kgrad[:, row_count:] + back_keys
    value_grad = near_vgrad[:, row_count:] + back_values
    segment_grads = []
    for (
        branch_index,
        chosen,
        picked_query,
        picked_key,
        picked_value,
        picked_grad,
        segment_keys,
        segment_values,
        seg_scores,
    ) in branches:
        seg_log = pick_rows(log_total, chosen)
        seg_inner = pick_rows(inner, chosen)
        part_query, segment_kgrad, segment_vgrad = block_grads(
            seg_scores, picked_query, segment_keys, segment_values, picked_grad, seg_log, seg_inner
        )
        query_grad = query_grad + spread_rows(part_query, chosen, 0.0)
        segment_grads.append((2 * branch_index + 1, (segment_kgrad, segment_vgrad)))
    owned = reduce_all(segment_grads, seq_index)
    for branch_entry, (own_kgrad, own_vgrad) in zip(branches, owned):
        chosen = branch_entry[1]
        key_grad = key_grad + spread_rows(own_kgrad, chosen, 0.0)
        value_grad = value_grad + spread_rows(own_vgrad, chosen, 0.0)
    flat = (row_count, head_count * HDIM)

    def to_rows(head_major):
        return head_major.astype(jnp.bfloat16).transpose(1, 0, 2).reshape(flat)

    return (to_rows(query_grad), to_rows(key_grad), to_rows(value_grad))


def solution(mesh):
    return jax.shard_map(
        per_device,
        mesh=mesh,
        in_specs=(
            P("seq", "head"),
            P("head", None),
            P("seq", "head"),
            P("seq", "head"),
            P("seq", "head"),
            P(None, "head"),
        ),
        out_specs=(P("seq", "head"), P("seq", "head"), P("seq", "head")),
        check_vma=False,
    )
```

```python
import jax
import jax.numpy as jnp
from jax import lax
from jax.sharding import PartitionSpec as P

HDIM = 128


def partner(shard, axis, stride):
    return lax.ppermute(shard, axis, [(i, i ^ 1 << stride) for i in range(lax.axis_size(axis))])


def shifted(value, axis, steps):
    count = lax.axis_size(axis)
    initial, last = (max(0, -steps), min(count, count - steps))
    return lax.ppermute(value, axis, [(source, source + steps) for source in range(initial, last)])


def pick_rows(block, chosen):
    dilation = chosen.shape[0]
    head_count = block.shape[0]
    shaped = block.reshape((head_count, block.shape[1] // dilation, dilation) + block.shape[2:])
    widened = chosen.T.reshape((head_count, 1, dilation) + (1,) * (block.ndim - 2))
    return jnp.sum(jnp.where(widened, shaped, jnp.zeros((), block.dtype)), axis=2)


def spread_rows(picked, chosen, filler):
    dilation = chosen.shape[0]
    head_count = picked.shape[0]
    widened = chosen.T.reshape((head_count, 1, dilation) + (1,) * (picked.ndim - 2))
    placed = jnp.where(widened, picked[:, :, None], jnp.asarray(filler, picked.dtype))
    return placed.reshape((head_count, picked.shape[1] * dilation) + picked.shape[2:])


def block_scores(query_rows, key_rows, key_live):
    scores = jnp.einsum(
        "hqd,hkd->hqk", query_rows, key_rows, preferred_element_type=jnp.float32
    ) * HDIM ** (-0.5)
    return jnp.where(key_live[None, None, :], scores, -jnp.inf)


def block_stats(scores):
    peak = jnp.max(scores, axis=2)
    total = jnp.sum(jnp.exp(scores - peak[:, :, None]), axis=2)
    return (peak, total)


def block_output(scores, value_rows, log_total):
    probs = jnp.exp(scores - log_total[:, :, None])
    weights = probs.astype(jnp.bfloat16)
    return jnp.einsum("hqk,hkd->hqd", weights, value_rows, preferred_element_type=jnp.float32)


def block_grads(scores, query_rows, key_rows, value_rows, out_grad, log_total, inner):
    probs = jnp.exp(scores - log_total[:, :, None])
    weights = probs.astype(jnp.bfloat16)
    flow = jnp.einsum("hqd,hkd->hqk", out_grad, value_rows, preferred_element_type=jnp.float32)
    slope = (probs * (flow - inner[:, :, None])).astype(jnp.bfloat16)
    scale = HDIM ** (-0.5)
    query_part = (
        jnp.einsum("hqk,hkd->hqd", slope, key_rows, preferred_element_type=jnp.float32) * scale
    )
    key_part = (
        jnp.einsum("hqk,hqd->hkd", slope, query_rows, preferred_element_type=jnp.float32) * scale
    )
    value_part = jnp.einsum("hqk,hqd->hkd", weights, out_grad, preferred_element_type=jnp.float32)
    return (query_part, key_part, value_part)


def exchange(arrays, bit_pos):
    sizes = [array.shape[1] for array in arrays]
    packed = jnp.concatenate(arrays, 1)
    arrived = partner(packed, "seq", bit_pos)
    cuts = [sum(sizes[: index + 1]) for index in range(len(sizes) - 1)]
    return jnp.split(arrived, cuts, axis=1)


def collect_all(groups, seq_index):
    steps_total = max(steps for steps, _ in groups)
    groups = [(steps, list(parts)) for steps, parts in groups]
    for bit_pos in reversed(range(steps_total)):
        active = [index for index, (steps, _) in enumerate(groups) if steps > bit_pos]
        sending = [part for index in active for part in groups[index][1]]
        arrived = exchange(sending, bit_pos)
        upper = seq_index // 2**bit_pos % 2 == 1
        at = 0
        for index in active:
            parts = groups[index][1]
            merged = []
            for own_part in parts:
                far_part = arrived[at]
                at += 1
                merged.append(
                    jnp.where(
                        upper,
                        jnp.concatenate([far_part, own_part], 1),
                        jnp.concatenate([own_part, far_part], 1),
                    )
                )
            groups[index] = (groups[index][0], merged)
    return [parts for _, parts in groups]


def reduce_all(groups, seq_index):
    steps_total = max(steps for steps, _ in groups)
    groups = [(steps, list(parts)) for steps, parts in groups]
    for bit_pos in range(steps_total):
        active = [index for index, (steps, _) in enumerate(groups) if steps > bit_pos]
        upper = seq_index // 2**bit_pos % 2 == 1
        sending = []
        keeping = []
        for index in active:
            for whole_part in groups[index][1]:
                half_rows = whole_part.shape[1] // 2
                sending.append(
                    jnp.where(upper, whole_part[:, :half_rows], whole_part[:, half_rows:])
                )
                keeping.append(
                    jnp.where(upper, whole_part[:, half_rows:], whole_part[:, :half_rows])
                )
        arrived = exchange([part.astype(jnp.bfloat16) for part in sending], bit_pos)
        at = 0
        for index in active:
            count = len(groups[index][1])
            groups[index] = (
                groups[index][0],
                [
                    kept + came.astype(jnp.float32)
                    for kept, came in zip(keeping[at : at + count], arrived[at : at + count])
                ],
            )
            at += count
    return [parts for _, parts in groups]


def ring_gather(block, axis):
    count = lax.axis_size(axis)
    own = lax.axis_index(axis)
    pieces = [block] + [
        lax.ppermute(block, axis, [(source, (source + step) % count) for source in range(count)])
        for step in range(1, count)
    ]
    stacked = jnp.stack(pieces)
    ordered = jnp.take(stacked, (own - jnp.arange(count)) % count, axis=0)
    return ordered.transpose(1, 0, 2).reshape(block.shape[0], count * block.shape[1])


def per_device(grad_out, out_weight, queries, keys, values, offsets):
    row_count = queries.shape[0]
    head_count = queries.shape[1] // HDIM
    branch_count = offsets.shape[0]
    view = (row_count, head_count, HDIM)

    def to_heads(flat_rows):
        return flat_rows.reshape(view).transpose(1, 0, 2)

    query_local = to_heads(queries)
    key_local = to_heads(keys)
    value_local = to_heads(values)
    seq_index = lax.axis_index("seq")
    prior_rows = shifted(jnp.concatenate([keys, values], 1), "seq", 1)
    prior_keys, prior_values = jnp.split(prior_rows, 2, axis=1)
    near_keys = jnp.concatenate([to_heads(prior_keys), key_local], 1)
    near_values = jnp.concatenate([to_heads(prior_values), value_local], 1)
    near_live = jnp.concatenate(
        [jnp.full((row_count,), seq_index > 0), jnp.ones((row_count,), jnp.bool_)]
    )
    picked_all = []
    for branch_index in range(1, branch_count + 1):
        dilation = 4**branch_index
        chosen = jnp.arange(dilation)[:, None] == offsets[branch_index - 1][None, :]
        picked_all.append(
            (
                chosen,
                pick_rows(query_local, chosen),
                pick_rows(key_local, chosen),
                pick_rows(value_local, chosen),
            )
        )
    gathered = collect_all(
        [(2 * index + 1, (entry[2], entry[3])) for index, entry in enumerate(picked_all, 1)],
        seq_index,
    )
    gathered_grad, _ = lax.optimization_barrier((ring_gather(grad_out, "head"), gathered[-1][0]))
    attn_flat = lax.dot_general(
        gathered_grad,
        out_weight,
        (((1,), (1,)), ((), ())),
        preferred_element_type=jnp.float32,
    )
    attn_grad = to_heads(attn_flat.astype(jnp.bfloat16))
    branches = []
    for branch_index in range(1, branch_count + 1):
        chosen, picked_query, picked_key, picked_value = picked_all[branch_index - 1]
        picked_grad = pick_rows(attn_grad, chosen)
        segment_keys, segment_values = gathered[branch_index - 1]
        segment_live = jnp.ones((segment_keys.shape[1],), jnp.bool_)
        seg_scores = block_scores(picked_query, segment_keys, segment_live)
        branches.append(
            (
                branch_index,
                chosen,
                picked_query,
                picked_key,
                picked_value,
                picked_grad,
                segment_keys,
                segment_values,
                seg_scores,
            )
        )
    near_scores = block_scores(query_local, near_keys, near_live)
    near_peak, near_total = block_stats(near_scores)
    peak = near_peak
    branch_stats = []
    for branch_entry in branches:
        chosen = branch_entry[1]
        seg_peak, seg_total = block_stats(branch_entry[8])
        branch_stats.append((seg_peak, seg_total))
        peak = jnp.maximum(peak, spread_rows(seg_peak, chosen, -jnp.inf))
    total = near_total * jnp.exp(near_peak - peak)
    for index_branch in range(len(branches)):
        chosen = branches[index_branch][1]
        seg_peak, seg_total = branch_stats[index_branch]
        total = total + spread_rows(
            seg_total * jnp.exp(seg_peak - pick_rows(peak, chosen)), chosen, 0.0
        )
    log_total = peak + jnp.log(total)
    output = block_output(near_scores, near_values, log_total)
    for (
        branch_index,
        chosen,
        picked_query,
        picked_key,
        picked_value,
        picked_grad,
        segment_keys,
        segment_values,
        seg_scores,
    ) in branches:
        seg_log = pick_rows(log_total, chosen)
        output = output + spread_rows(
            block_output(seg_scores, segment_values, seg_log), chosen, 0.0
        )
    inner = jnp.sum(attn_grad.astype(jnp.float32) * output, axis=2)
    near_qgrad, near_kgrad, near_vgrad = block_grads(
        near_scores, query_local, near_keys, near_values, attn_grad, log_total, inner
    )
    back_rows = shifted(
        jnp.concatenate([near_kgrad[:, :row_count], near_vgrad[:, :row_count]], 1).astype(
            jnp.bfloat16
        ),
        "seq",
        -1,
    )
    back_keys, back_values = jnp.split(back_rows.astype(jnp.float32), 2, axis=1)
    query_grad = near_qgrad
    key_grad = near_kgrad[:, row_count:] + back_keys
    value_grad = near_vgrad[:, row_count:] + back_values
    segment_grads = []
    for (
        branch_index,
        chosen,
        picked_query,
        picked_key,
        picked_value,
        picked_grad,
        segment_keys,
        segment_values,
        seg_scores,
    ) in branches:
        seg_log = pick_rows(log_total, chosen)
        seg_inner = pick_rows(inner, chosen)
        part_query, segment_kgrad, segment_vgrad = block_grads(
            seg_scores, picked_query, segment_keys, segment_values, picked_grad, seg_log, seg_inner
        )
        query_grad = query_grad + spread_rows(part_query, chosen, 0.0)
        segment_grads.append((2 * branch_index + 1, (segment_kgrad, segment_vgrad)))
    owned = reduce_all(segment_grads, seq_index)
    for branch_entry, (own_kgrad, own_vgrad) in zip(branches, owned):
        chosen = branch_entry[1]
        key_grad = key_grad + spread_rows(own_kgrad, chosen, 0.0)
        value_grad = value_grad + spread_rows(own_vgrad, chosen, 0.0)
    flat = (row_count, head_count * HDIM)

    def to_rows(head_major):
        return head_major.astype(jnp.bfloat16).transpose(1, 0, 2).reshape(flat)

    return (to_rows(query_grad), to_rows(key_grad), to_rows(value_grad))


def solution(mesh):
    return jax.shard_map(
        per_device,
        mesh=mesh,
        in_specs=(
            P("seq", "head"),
            P("head", None),
            P("seq", "head"),
            P("seq", "head"),
            P("seq", "head"),
            P(None, "head"),
        ),
        out_specs=(P("seq", "head"), P("seq", "head"), P("seq", "head")),
        check_vma=False,
    )
```

```python
import jax
import jax.numpy as jnp
from jax import lax
from jax.sharding import PartitionSpec as P

HDIM = 128


def partner(shard, axis, stride):
    return lax.ppermute(shard, axis, [(i, i ^ 1 << stride) for i in range(lax.axis_size(axis))])


def shifted(value, axis, steps):
    count = lax.axis_size(axis)
    initial, last = (max(0, -steps), min(count, count - steps))
    return lax.ppermute(value, axis, [(source, source + steps) for source in range(initial, last)])


def pick_rows(block, chosen):
    dilation = chosen.shape[0]
    head_count = block.shape[0]
    shaped = block.reshape((head_count, block.shape[1] // dilation, dilation) + block.shape[2:])
    widened = chosen.T.reshape((head_count, 1, dilation) + (1,) * (block.ndim - 2))
    return jnp.sum(jnp.where(widened, shaped, jnp.zeros((), block.dtype)), axis=2)


def spread_rows(picked, chosen, filler):
    dilation = chosen.shape[0]
    head_count = picked.shape[0]
    widened = chosen.T.reshape((head_count, 1, dilation) + (1,) * (picked.ndim - 2))
    placed = jnp.where(widened, picked[:, :, None], jnp.asarray(filler, picked.dtype))
    return placed.reshape((head_count, picked.shape[1] * dilation) + picked.shape[2:])


def block_scores(query_rows, key_rows, key_live):
    scores = jnp.einsum(
        "hqd,hkd->hqk", query_rows, key_rows, preferred_element_type=jnp.float32
    ) * HDIM ** (-0.5)
    return jnp.where(key_live[None, None, :], scores, -jnp.inf)


def block_stats(scores):
    peak = jnp.max(scores, axis=2)
    total = jnp.sum(jnp.exp(scores - peak[:, :, None]), axis=2)
    return (peak, total)


def block_output(scores, value_rows, log_total):
    probs = jnp.exp(scores - log_total[:, :, None])
    weights = probs.astype(jnp.bfloat16)
    return jnp.einsum("hqk,hkd->hqd", weights, value_rows, preferred_element_type=jnp.float32)


def block_grads(scores, query_rows, key_rows, value_rows, out_grad, log_total, inner):
    probs = jnp.exp(scores - log_total[:, :, None])
    weights = probs.astype(jnp.bfloat16)
    flow = jnp.einsum("hqd,hkd->hqk", out_grad, value_rows, preferred_element_type=jnp.float32)
    slope = (probs * (flow - inner[:, :, None])).astype(jnp.bfloat16)
    scale = HDIM ** (-0.5)
    query_part = (
        jnp.einsum("hqk,hkd->hqd", slope, key_rows, preferred_element_type=jnp.float32) * scale
    )
    key_part = (
        jnp.einsum("hqk,hqd->hkd", slope, query_rows, preferred_element_type=jnp.float32) * scale
    )
    value_part = jnp.einsum("hqk,hqd->hkd", weights, out_grad, preferred_element_type=jnp.float32)
    return (query_part, key_part, value_part)


def exchange(arrays, bit_pos):
    sizes = [array.shape[1] for array in arrays]
    packed = jnp.concatenate(arrays, 1)
    arrived = partner(packed, "seq", bit_pos)
    cuts = [sum(sizes[: index + 1]) for index in range(len(sizes) - 1)]
    return jnp.split(arrived, cuts, axis=1)


def collect_all(groups, seq_index, tied):
    steps_total = max(steps for steps, _ in groups)
    groups = [(steps, list(parts)) for steps, parts in groups]
    for bit_pos in reversed(range(steps_total)):
        active = [index for index, (steps, _) in enumerate(groups) if steps > bit_pos]
        sending = [part for index in active for part in groups[index][1]]
        arrived = exchange(sending, bit_pos)
        if bit_pos == steps_total - 1:
            tied, _ = lax.optimization_barrier((tied, arrived[0]))
        upper = seq_index // 2**bit_pos % 2 == 1
        at = 0
        for index in active:
            parts = groups[index][1]
            merged = []
            for own_part in parts:
                far_part = arrived[at]
                at += 1
                merged.append(
                    jnp.where(
                        upper,
                        jnp.concatenate([far_part, own_part], 1),
                        jnp.concatenate([own_part, far_part], 1),
                    )
                )
            groups[index] = (groups[index][0], merged)
    return ([parts for _, parts in groups], tied)


def reduce_all(groups, seq_index):
    steps_total = max(steps for steps, _ in groups)
    groups = [(steps, list(parts)) for steps, parts in groups]
    for bit_pos in range(steps_total):
        active = [index for index, (steps, _) in enumerate(groups) if steps > bit_pos]
        upper = seq_index // 2**bit_pos % 2 == 1
        sending = []
        keeping = []
        for index in active:
            for whole_part in groups[index][1]:
                half_rows = whole_part.shape[1] // 2
                sending.append(
                    jnp.where(upper, whole_part[:, :half_rows], whole_part[:, half_rows:])
                )
                keeping.append(
                    jnp.where(upper, whole_part[:, half_rows:], whole_part[:, :half_rows])
                )
        arrived = exchange([part.astype(jnp.bfloat16) for part in sending], bit_pos)
        at = 0
        for index in active:
            count = len(groups[index][1])
            groups[index] = (
                groups[index][0],
                [
                    kept + came.astype(jnp.float32)
                    for kept, came in zip(keeping[at : at + count], arrived[at : at + count])
                ],
            )
            at += count
    return [parts for _, parts in groups]


def ring_gather(block, axis):
    count = lax.axis_size(axis)
    own = lax.axis_index(axis)
    pieces = [block] + [
        lax.ppermute(block, axis, [(source, (source + step) % count) for source in range(count)])
        for step in range(1, count)
    ]
    stacked = jnp.stack(pieces)
    ordered = jnp.take(stacked, (own - jnp.arange(count)) % count, axis=0)
    return ordered.transpose(1, 0, 2).reshape(block.shape[0], count * block.shape[1])


def per_device(grad_out, out_weight, queries, keys, values, offsets):
    row_count = queries.shape[0]
    head_count = queries.shape[1] // HDIM
    branch_count = offsets.shape[0]
    view = (row_count, head_count, HDIM)

    def to_heads(flat_rows):
        return flat_rows.reshape(view).transpose(1, 0, 2)

    query_local = to_heads(queries)
    key_local = to_heads(keys)
    value_local = to_heads(values)
    seq_index = lax.axis_index("seq")
    prior_rows = shifted(jnp.concatenate([keys, values], 1), "seq", 1)
    prior_keys, prior_values = jnp.split(prior_rows, 2, axis=1)
    near_keys = jnp.concatenate([to_heads(prior_keys), key_local], 1)
    near_values = jnp.concatenate([to_heads(prior_values), value_local], 1)
    near_live = jnp.concatenate(
        [jnp.full((row_count,), seq_index > 0), jnp.ones((row_count,), jnp.bool_)]
    )
    picked_all = []
    for branch_index in range(1, branch_count + 1):
        dilation = 4**branch_index
        chosen = jnp.arange(dilation)[:, None] == offsets[branch_index - 1][None, :]
        picked_all.append(
            (
                chosen,
                pick_rows(query_local, chosen),
                pick_rows(key_local, chosen),
                pick_rows(value_local, chosen),
            )
        )
    gathered, late_grad = collect_all(
        [(2 * index + 1, (entry[2], entry[3])) for index, entry in enumerate(picked_all, 1)],
        seq_index,
        grad_out,
    )
    gathered_grad, _ = lax.optimization_barrier((ring_gather(late_grad, "head"), gathered[-1][0]))
    attn_flat = lax.dot_general(
        gathered_grad,
        out_weight,
        (((1,), (1,)), ((), ())),
        preferred_element_type=jnp.float32,
    )
    attn_grad = to_heads(attn_flat.astype(jnp.bfloat16))
    branches = []
    for branch_index in range(1, branch_count + 1):
        chosen, picked_query, picked_key, picked_value = picked_all[branch_index - 1]
        picked_grad = pick_rows(attn_grad, chosen)
        segment_keys, segment_values = gathered[branch_index - 1]
        segment_live = jnp.ones((segment_keys.shape[1],), jnp.bool_)
        seg_scores = block_scores(picked_query, segment_keys, segment_live)
        branches.append(
            (
                branch_index,
                chosen,
                picked_query,
                picked_key,
                picked_value,
                picked_grad,
                segment_keys,
                segment_values,
                seg_scores,
            )
        )
    near_scores = block_scores(query_local, near_keys, near_live)
    near_peak, near_total = block_stats(near_scores)
    peak = near_peak
    branch_stats = []
    for branch_entry in branches:
        chosen = branch_entry[1]
        seg_peak, seg_total = block_stats(branch_entry[8])
        branch_stats.append((seg_peak, seg_total))
        peak = jnp.maximum(peak, spread_rows(seg_peak, chosen, -jnp.inf))
    total = near_total * jnp.exp(near_peak - peak)
    for index_branch in range(len(branches)):
        chosen = branches[index_branch][1]
        seg_peak, seg_total = branch_stats[index_branch]
        total = total + spread_rows(
            seg_total * jnp.exp(seg_peak - pick_rows(peak, chosen)), chosen, 0.0
        )
    log_total = peak + jnp.log(total)
    output = block_output(near_scores, near_values, log_total)
    for (
        branch_index,
        chosen,
        picked_query,
        picked_key,
        picked_value,
        picked_grad,
        segment_keys,
        segment_values,
        seg_scores,
    ) in branches:
        seg_log = pick_rows(log_total, chosen)
        output = output + spread_rows(
            block_output(seg_scores, segment_values, seg_log), chosen, 0.0
        )
    inner = jnp.sum(attn_grad.astype(jnp.float32) * output, axis=2)
    near_qgrad, near_kgrad, near_vgrad = block_grads(
        near_scores, query_local, near_keys, near_values, attn_grad, log_total, inner
    )
    back_rows = shifted(
        jnp.concatenate([near_kgrad[:, :row_count], near_vgrad[:, :row_count]], 1).astype(
            jnp.bfloat16
        ),
        "seq",
        -1,
    )
    back_keys, back_values = jnp.split(back_rows.astype(jnp.float32), 2, axis=1)
    query_grad = near_qgrad
    key_grad = near_kgrad[:, row_count:] + back_keys
    value_grad = near_vgrad[:, row_count:] + back_values
    segment_grads = []
    for (
        branch_index,
        chosen,
        picked_query,
        picked_key,
        picked_value,
        picked_grad,
        segment_keys,
        segment_values,
        seg_scores,
    ) in branches:
        seg_log = pick_rows(log_total, chosen)
        seg_inner = pick_rows(inner, chosen)
        part_query, segment_kgrad, segment_vgrad = block_grads(
            seg_scores, picked_query, segment_keys, segment_values, picked_grad, seg_log, seg_inner
        )
        query_grad = query_grad + spread_rows(part_query, chosen, 0.0)
        segment_grads.append((2 * branch_index + 1, (segment_kgrad, segment_vgrad)))
    owned = reduce_all(segment_grads, seq_index)
    for branch_entry, (own_kgrad, own_vgrad) in zip(branches, owned):
        chosen = branch_entry[1]
        key_grad = key_grad + spread_rows(own_kgrad, chosen, 0.0)
        value_grad = value_grad + spread_rows(own_vgrad, chosen, 0.0)
    flat = (row_count, head_count * HDIM)

    def to_rows(head_major):
        return head_major.astype(jnp.bfloat16).transpose(1, 0, 2).reshape(flat)

    return (to_rows(query_grad), to_rows(key_grad), to_rows(value_grad))


def solution(mesh):
    return jax.shard_map(
        per_device,
        mesh=mesh,
        in_specs=(
            P("seq", "head"),
            P("head", None),
            P("seq", "head"),
            P("seq", "head"),
            P("seq", "head"),
            P(None, "head"),
        ),
        out_specs=(P("seq", "head"), P("seq", "head"), P("seq", "head")),
        check_vma=False,
    )
```

```python
import jax
import jax.numpy as jnp
from jax import lax
from jax.sharding import PartitionSpec as P

HDIM = 128


def partner(shard, axis, stride):
    return lax.ppermute(shard, axis, [(i, i ^ 1 << stride) for i in range(lax.axis_size(axis))])


def shifted(value, axis, steps):
    count = lax.axis_size(axis)
    initial, last = (max(0, -steps), min(count, count - steps))
    return lax.ppermute(value, axis, [(source, source + steps) for source in range(initial, last)])


def pick_rows(block, chosen):
    dilation = chosen.shape[0]
    head_count = block.shape[0]
    shaped = block.reshape((head_count, block.shape[1] // dilation, dilation) + block.shape[2:])
    widened = chosen.T.reshape((head_count, 1, dilation) + (1,) * (block.ndim - 2))
    return jnp.sum(jnp.where(widened, shaped, jnp.zeros((), block.dtype)), axis=2)


def pick_flat(flat_rows, chosen):
    dilation, head_count = chosen.shape
    shaped = flat_rows.reshape(flat_rows.shape[0] // dilation, dilation, head_count, HDIM)
    widened = chosen.reshape(1, dilation, head_count, 1)
    picked = jnp.sum(jnp.where(widened, shaped, jnp.zeros((), flat_rows.dtype)), axis=1)
    return picked.transpose(1, 0, 2)


def spread_rows(picked, chosen, filler):
    dilation = chosen.shape[0]
    head_count = picked.shape[0]
    widened = chosen.T.reshape((head_count, 1, dilation) + (1,) * (picked.ndim - 2))
    placed = jnp.where(widened, picked[:, :, None], jnp.asarray(filler, picked.dtype))
    return placed.reshape((head_count, picked.shape[1] * dilation) + picked.shape[2:])


def block_scores(query_rows, key_rows, key_live):
    scores = jnp.einsum(
        "hqd,hkd->hqk", query_rows, key_rows, preferred_element_type=jnp.float32
    ) * HDIM ** (-0.5)
    return jnp.where(key_live[None, None, :], scores, -jnp.inf)


def block_stats(scores):
    peak = jnp.max(scores, axis=2)
    total = jnp.sum(jnp.exp(scores - peak[:, :, None]), axis=2)
    return (peak, total)


def block_output(scores, value_rows, log_total):
    probs = jnp.exp(scores - log_total[:, :, None])
    weights = probs.astype(jnp.bfloat16)
    return jnp.einsum("hqk,hkd->hqd", weights, value_rows, preferred_element_type=jnp.float32)


def block_grads(scores, query_rows, key_rows, value_rows, out_grad, log_total, inner):
    probs = jnp.exp(scores - log_total[:, :, None])
    weights = probs.astype(jnp.bfloat16)
    flow = jnp.einsum("hqd,hkd->hqk", out_grad, value_rows, preferred_element_type=jnp.float32)
    slope = (probs * (flow - inner[:, :, None])).astype(jnp.bfloat16)
    scale = HDIM ** (-0.5)
    query_part = (
        jnp.einsum("hqk,hkd->hqd", slope, key_rows, preferred_element_type=jnp.float32) * scale
    )
    key_part = (
        jnp.einsum("hqk,hqd->hkd", slope, query_rows, preferred_element_type=jnp.float32) * scale
    )
    value_part = jnp.einsum("hqk,hqd->hkd", weights, out_grad, preferred_element_type=jnp.float32)
    return (query_part, key_part, value_part)


def exchange(arrays, bit_pos):
    sizes = [array.shape[1] for array in arrays]
    packed = jnp.concatenate(arrays, 1)
    arrived = partner(packed, "seq", bit_pos)
    cuts = [sum(sizes[: index + 1]) for index in range(len(sizes) - 1)]
    return jnp.split(arrived, cuts, axis=1)


def collect_all(groups, seq_index, tied, make_last):
    steps_total = max(steps for steps, _ in groups)
    groups = [(steps, list(parts)) for steps, parts in groups]
    last = None
    for bit_pos in reversed(range(steps_total)):
        active = [index for index, (steps, _) in enumerate(groups) if steps > bit_pos]
        sending = [part for index in active for part in groups[index][1]]
        if bit_pos == 0:
            sending, last = lax.optimization_barrier((sending, make_last()))
        arrived = exchange(sending, bit_pos)
        if bit_pos == steps_total - 1:
            tied, _ = lax.optimization_barrier((tied, arrived[0]))
        upper = seq_index // 2**bit_pos % 2 == 1
        at = 0
        for index in active:
            parts = groups[index][1]
            merged = []
            for own_part in parts:
                far_part = arrived[at]
                at += 1
                merged.append(
                    jnp.where(
                        upper,
                        jnp.concatenate([far_part, own_part], 1),
                        jnp.concatenate([own_part, far_part], 1),
                    )
                )
            groups[index] = (groups[index][0], merged)
    return ([parts for _, parts in groups], tied, last)


def reduce_all(groups, seq_index):
    steps_total = max(steps for steps, _ in groups)
    groups = [(steps, list(parts)) for steps, parts in groups]
    for bit_pos in range(steps_total):
        active = [index for index, (steps, _) in enumerate(groups) if steps > bit_pos]
        upper = seq_index // 2**bit_pos % 2 == 1
        sending = []
        keeping = []
        for index in active:
            for whole_part in groups[index][1]:
                half_rows = whole_part.shape[1] // 2
                sending.append(
                    jnp.where(upper, whole_part[:, :half_rows], whole_part[:, half_rows:])
                )
                keeping.append(
                    jnp.where(upper, whole_part[:, half_rows:], whole_part[:, :half_rows])
                )
        arrived = exchange([part.astype(jnp.bfloat16) for part in sending], bit_pos)
        at = 0
        for index in active:
            count = len(groups[index][1])
            groups[index] = (
                groups[index][0],
                [
                    kept + came.astype(jnp.float32)
                    for kept, came in zip(keeping[at : at + count], arrived[at : at + count])
                ],
            )
            at += count
    return [parts for _, parts in groups]


def ring_gather(block, axis):
    count = lax.axis_size(axis)
    own = lax.axis_index(axis)
    pieces = [block] + [
        lax.ppermute(block, axis, [(source, (source + step) % count) for source in range(count)])
        for step in range(1, count)
    ]
    stacked = jnp.stack(pieces)
    ordered = jnp.take(stacked, (own - jnp.arange(count)) % count, axis=0)
    return ordered.transpose(1, 0, 2).reshape(block.shape[0], count * block.shape[1])


def per_device(grad_out, out_weight, queries, keys, values, offsets):
    row_count = queries.shape[0]
    head_count = queries.shape[1] // HDIM
    branch_count = offsets.shape[0]
    view = (row_count, head_count, HDIM)

    def to_heads(flat_rows):
        return flat_rows.reshape(view).transpose(1, 0, 2)

    query_local = to_heads(queries)
    key_local = to_heads(keys)
    value_local = to_heads(values)
    seq_index = lax.axis_index("seq")
    prior_rows = shifted(jnp.concatenate([keys, values], 1), "seq", 1)
    prior_keys, prior_values = jnp.split(prior_rows, 2, axis=1)
    near_keys = jnp.concatenate([to_heads(prior_keys), key_local], 1)
    near_values = jnp.concatenate([to_heads(prior_values), value_local], 1)
    near_live = jnp.concatenate(
        [jnp.full((row_count,), seq_index > 0), jnp.ones((row_count,), jnp.bool_)]
    )
    picked_all = []
    for branch_index in range(1, branch_count + 1):
        dilation = 4**branch_index
        chosen = jnp.arange(dilation)[:, None] == offsets[branch_index - 1][None, :]
        picked_all.append(
            (
                chosen,
                pick_rows(query_local, chosen),
                pick_flat(keys, chosen),
                pick_flat(values, chosen),
            )
        )

    def near_forward():
        near_scores = block_scores(query_local, near_keys, near_live)
        return (near_scores,) + block_stats(near_scores)

    gathered, late_grad, (near_scores, near_peak, near_total) = collect_all(
        [(2 * index + 1, (entry[2], entry[3])) for index, entry in enumerate(picked_all, 1)],
        seq_index,
        grad_out,
        near_forward,
    )
    gathered_grad, _ = lax.optimization_barrier((ring_gather(late_grad, "head"), gathered[-1][0]))
    attn_flat = lax.dot_general(
        gathered_grad,
        out_weight,
        (((1,), (1,)), ((), ())),
        preferred_element_type=jnp.float32,
    )
    attn_grad = to_heads(attn_flat.astype(jnp.bfloat16))
    branches = []
    for branch_index in range(1, branch_count + 1):
        chosen, picked_query, picked_key, picked_value = picked_all[branch_index - 1]
        picked_grad = pick_rows(attn_grad, chosen)
        segment_keys, segment_values = gathered[branch_index - 1]
        segment_live = jnp.ones((segment_keys.shape[1],), jnp.bool_)
        seg_scores = block_scores(picked_query, segment_keys, segment_live)
        branches.append(
            (
                branch_index,
                chosen,
                picked_query,
                picked_key,
                picked_value,
                picked_grad,
                segment_keys,
                segment_values,
                seg_scores,
            )
        )
    peak = near_peak
    branch_stats = []
    for branch_entry in branches:
        chosen = branch_entry[1]
        seg_peak, seg_total = block_stats(branch_entry[8])
        branch_stats.append((seg_peak, seg_total))
        peak = jnp.maximum(peak, spread_rows(seg_peak, chosen, -jnp.inf))
    total = near_total * jnp.exp(near_peak - peak)
    for index_branch in range(len(branches)):
        chosen = branches[index_branch][1]
        seg_peak, seg_total = branch_stats[index_branch]
        total = total + spread_rows(
            seg_total * jnp.exp(seg_peak - pick_rows(peak, chosen)), chosen, 0.0
        )
    log_total = peak + jnp.log(total)
    output = block_output(near_scores, near_values, log_total)
    for (
        branch_index,
        chosen,
        picked_query,
        picked_key,
        picked_value,
        picked_grad,
        segment_keys,
        segment_values,
        seg_scores,
    ) in branches:
        seg_log = pick_rows(log_total, chosen)
        output = output + spread_rows(
            block_output(seg_scores, segment_values, seg_log), chosen, 0.0
        )
    inner = jnp.sum(attn_grad.astype(jnp.float32) * output, axis=2)
    near_qgrad, near_kgrad, near_vgrad = block_grads(
        near_scores, query_local, near_keys, near_values, attn_grad, log_total, inner
    )
    back_rows = shifted(
        jnp.concatenate([near_kgrad[:, :row_count], near_vgrad[:, :row_count]], 1).astype(
            jnp.bfloat16
        ),
        "seq",
        -1,
    )
    back_keys, back_values = jnp.split(back_rows.astype(jnp.float32), 2, axis=1)
    query_grad = near_qgrad
    key_grad = near_kgrad[:, row_count:] + back_keys
    value_grad = near_vgrad[:, row_count:] + back_values
    segment_grads = []
    for (
        branch_index,
        chosen,
        picked_query,
        picked_key,
        picked_value,
        picked_grad,
        segment_keys,
        segment_values,
        seg_scores,
    ) in branches:
        seg_log = pick_rows(log_total, chosen)
        seg_inner = pick_rows(inner, chosen)
        part_query, segment_kgrad, segment_vgrad = block_grads(
            seg_scores, picked_query, segment_keys, segment_values, picked_grad, seg_log, seg_inner
        )
        query_grad = query_grad + spread_rows(part_query, chosen, 0.0)
        segment_grads.append((2 * branch_index + 1, (segment_kgrad, segment_vgrad)))
    owned = reduce_all(segment_grads, seq_index)
    for branch_entry, (own_kgrad, own_vgrad) in zip(branches, owned):
        chosen = branch_entry[1]
        key_grad = key_grad + spread_rows(own_kgrad, chosen, 0.0)
        value_grad = value_grad + spread_rows(own_vgrad, chosen, 0.0)
    flat = (row_count, head_count * HDIM)

    def to_rows(head_major):
        return head_major.astype(jnp.bfloat16).transpose(1, 0, 2).reshape(flat)

    return (to_rows(query_grad), to_rows(key_grad), to_rows(value_grad))


def solution(mesh):
    return jax.shard_map(
        per_device,
        mesh=mesh,
        in_specs=(
            P("seq", "head"),
            P("head", None),
            P("seq", "head"),
            P("seq", "head"),
            P("seq", "head"),
            P(None, "head"),
        ),
        out_specs=(P("seq", "head"), P("seq", "head"), P("seq", "head")),
        check_vma=False,
    )
```

```python
import jax
import jax.numpy as jnp
from jax import lax
from jax.sharding import PartitionSpec as P

HDIM = 128


def partner(shard, axis, stride):
    return lax.ppermute(shard, axis, [(i, i ^ 1 << stride) for i in range(lax.axis_size(axis))])


def shifted(value, axis, steps):
    count = lax.axis_size(axis)
    initial, last = (max(0, -steps), min(count, count - steps))
    return lax.ppermute(value, axis, [(source, source + steps) for source in range(initial, last)])


def pick_rows(block, chosen):
    dilation = chosen.shape[0]
    head_count = block.shape[0]
    shaped = block.reshape((head_count, block.shape[1] // dilation, dilation) + block.shape[2:])
    widened = chosen.T.reshape((head_count, 1, dilation) + (1,) * (block.ndim - 2))
    return jnp.sum(jnp.where(widened, shaped, jnp.zeros((), block.dtype)), axis=2)


def spread_rows(picked, chosen, filler):
    dilation = chosen.shape[0]
    head_count = picked.shape[0]
    widened = chosen.T.reshape((head_count, 1, dilation) + (1,) * (picked.ndim - 2))
    placed = jnp.where(widened, picked[:, :, None], jnp.asarray(filler, picked.dtype))
    return placed.reshape((head_count, picked.shape[1] * dilation) + picked.shape[2:])


def block_scores(query_rows, key_rows, key_live):
    scores = jnp.einsum(
        "hqd,hkd->hqk", query_rows, key_rows, preferred_element_type=jnp.float32
    ) * HDIM ** (-0.5)
    return jnp.where(key_live[None, None, :], scores, -jnp.inf)


def block_stats(scores):
    peak = jnp.max(scores, axis=2)
    total = jnp.sum(jnp.exp(scores - peak[:, :, None]), axis=2)
    return (peak, total)


def block_output(scores, value_rows, log_total):
    probs = jnp.exp(scores - log_total[:, :, None])
    weights = probs.astype(jnp.bfloat16)
    return jnp.einsum("hqk,hkd->hqd", weights, value_rows, preferred_element_type=jnp.float32)


def block_grads(scores, query_rows, key_rows, value_rows, out_grad, log_total, inner):
    probs = jnp.exp(scores - log_total[:, :, None])
    weights = probs.astype(jnp.bfloat16)
    flow = jnp.einsum("hqd,hkd->hqk", out_grad, value_rows, preferred_element_type=jnp.float32)
    slope = (probs * (flow - inner[:, :, None])).astype(jnp.bfloat16)
    scale = HDIM ** (-0.5)
    query_part = (
        jnp.einsum("hqk,hkd->hqd", slope, key_rows, preferred_element_type=jnp.float32) * scale
    )
    key_part = (
        jnp.einsum("hqk,hqd->hkd", slope, query_rows, preferred_element_type=jnp.float32) * scale
    )
    value_part = jnp.einsum("hqk,hqd->hkd", weights, out_grad, preferred_element_type=jnp.float32)
    return (query_part, key_part, value_part)


def exchange(arrays, bit_pos):
    sizes = [array.shape[1] for array in arrays]
    packed = jnp.concatenate(arrays, 1)
    arrived = partner(packed, "seq", bit_pos)
    cuts = [sum(sizes[: index + 1]) for index in range(len(sizes) - 1)]
    return jnp.split(arrived, cuts, axis=1)


def collect_all(groups, seq_index, tied):
    steps_total = max(steps for steps, _ in groups)
    groups = [(steps, list(parts)) for steps, parts in groups]
    for bit_pos in reversed(range(steps_total)):
        active = [index for index, (steps, _) in enumerate(groups) if steps > bit_pos]
        sending = [part for index in active for part in groups[index][1]]
        arrived = exchange(sending, bit_pos)
        if bit_pos == steps_total - 1:
            tied, _ = lax.optimization_barrier((tied, arrived[0]))
        upper = seq_index // 2**bit_pos % 2 == 1
        at = 0
        for index in active:
            parts = groups[index][1]
            merged = []
            for own_part in parts:
                far_part = arrived[at]
                at += 1
                merged.append(
                    jnp.where(
                        upper,
                        jnp.concatenate([far_part, own_part], 1),
                        jnp.concatenate([own_part, far_part], 1),
                    )
                )
            groups[index] = (groups[index][0], merged)
    return ([parts for _, parts in groups], tied)


def reduce_all(groups, seq_index, tied):
    steps_total = max(steps for steps, _ in groups)
    groups = [(steps, list(parts)) for steps, parts in groups]
    for bit_pos in range(steps_total):
        active = [index for index, (steps, _) in enumerate(groups) if steps > bit_pos]
        upper = seq_index // 2**bit_pos % 2 == 1
        sending = []
        keeping = []
        for index in active:
            for whole_part in groups[index][1]:
                half_rows = whole_part.shape[1] // 2
                sending.append(
                    jnp.where(upper, whole_part[:, :half_rows], whole_part[:, half_rows:])
                )
                keeping.append(
                    jnp.where(upper, whole_part[:, half_rows:], whole_part[:, :half_rows])
                )
        arrived = exchange([part.astype(jnp.bfloat16) for part in sending], bit_pos)
        if bit_pos == 0:
            tied, _ = lax.optimization_barrier((tied, arrived[0]))
        at = 0
        for index in active:
            count = len(groups[index][1])
            groups[index] = (
                groups[index][0],
                [
                    kept + came.astype(jnp.float32)
                    for kept, came in zip(keeping[at : at + count], arrived[at : at + count])
                ],
            )
            at += count
    return ([parts for _, parts in groups], tied)


def ring_gather(block, axis):
    count = lax.axis_size(axis)
    own = lax.axis_index(axis)
    pieces = [block] + [
        lax.ppermute(block, axis, [(source, (source + step) % count) for source in range(count)])
        for step in range(1, count)
    ]
    stacked = jnp.stack(pieces)
    ordered = jnp.take(stacked, (own - jnp.arange(count)) % count, axis=0)
    return ordered.transpose(1, 0, 2).reshape(block.shape[0], count * block.shape[1])


def per_device(grad_out, out_weight, queries, keys, values, offsets):
    row_count = queries.shape[0]
    head_count = queries.shape[1] // HDIM
    branch_count = offsets.shape[0]
    view = (row_count, head_count, HDIM)

    def to_heads(flat_rows):
        return flat_rows.reshape(view).transpose(1, 0, 2)

    query_local = to_heads(queries)
    key_local = to_heads(keys)
    value_local = to_heads(values)
    seq_index = lax.axis_index("seq")
    prior_rows = shifted(jnp.concatenate([keys, values], 1), "seq", 1)
    prior_keys, prior_values = jnp.split(prior_rows, 2, axis=1)
    near_keys = jnp.concatenate([to_heads(prior_keys), key_local], 1)
    near_values = jnp.concatenate([to_heads(prior_values), value_local], 1)
    near_live = jnp.concatenate(
        [jnp.full((row_count,), seq_index > 0), jnp.ones((row_count,), jnp.bool_)]
    )
    picked_all = []
    for branch_index in range(1, branch_count + 1):
        dilation = 4**branch_index
        chosen = jnp.arange(dilation)[:, None] == offsets[branch_index - 1][None, :]
        picked_all.append(
            (
                chosen,
                pick_rows(query_local, chosen),
                pick_rows(key_local, chosen),
                pick_rows(value_local, chosen),
            )
        )
    gathered, late_grad = collect_all(
        [(2 * index + 1, (entry[2], entry[3])) for index, entry in enumerate(picked_all, 1)],
        seq_index,
        grad_out,
    )
    gathered_grad, _ = lax.optimization_barrier((ring_gather(late_grad, "head"), gathered[-1][0]))
    attn_flat = lax.dot_general(
        gathered_grad,
        out_weight,
        (((1,), (1,)), ((), ())),
        preferred_element_type=jnp.float32,
    )
    attn_grad = to_heads(attn_flat.astype(jnp.bfloat16))
    branches = []
    for branch_index in range(1, branch_count + 1):
        chosen, picked_query, picked_key, picked_value = picked_all[branch_index - 1]
        picked_grad = pick_rows(attn_grad, chosen)
        segment_keys, segment_values = gathered[branch_index - 1]
        segment_live = jnp.ones((segment_keys.shape[1],), jnp.bool_)
        seg_scores = block_scores(picked_query, segment_keys, segment_live)
        branches.append(
            (
                branch_index,
                chosen,
                picked_query,
                picked_key,
                picked_value,
                picked_grad,
                segment_keys,
                segment_values,
                seg_scores,
            )
        )
    near_scores = block_scores(query_local, near_keys, near_live)
    near_peak, near_total = block_stats(near_scores)
    peak = near_peak
    branch_stats = []
    for branch_entry in branches:
        chosen = branch_entry[1]
        seg_peak, seg_total = block_stats(branch_entry[8])
        branch_stats.append((seg_peak, seg_total))
        peak = jnp.maximum(peak, spread_rows(seg_peak, chosen, -jnp.inf))
    total = near_total * jnp.exp(near_peak - peak)
    for index_branch in range(len(branches)):
        chosen = branches[index_branch][1]
        seg_peak, seg_total = branch_stats[index_branch]
        total = total + spread_rows(
            seg_total * jnp.exp(seg_peak - pick_rows(peak, chosen)), chosen, 0.0
        )
    log_total = peak + jnp.log(total)
    output = block_output(near_scores, near_values, log_total)
    for (
        branch_index,
        chosen,
        picked_query,
        picked_key,
        picked_value,
        picked_grad,
        segment_keys,
        segment_values,
        seg_scores,
    ) in branches:
        seg_log = pick_rows(log_total, chosen)
        output = output + spread_rows(
            block_output(seg_scores, segment_values, seg_log), chosen, 0.0
        )
    inner = jnp.sum(attn_grad.astype(jnp.float32) * output, axis=2)
    segment_grads = []
    branch_qgrad = jnp.zeros(query_local.shape, jnp.float32)
    for (
        branch_index,
        chosen,
        picked_query,
        picked_key,
        picked_value,
        picked_grad,
        segment_keys,
        segment_values,
        seg_scores,
    ) in branches:
        seg_log = pick_rows(log_total, chosen)
        seg_inner = pick_rows(inner, chosen)
        part_query, segment_kgrad, segment_vgrad = block_grads(
            seg_scores, picked_query, segment_keys, segment_values, picked_grad, seg_log, seg_inner
        )
        branch_qgrad = branch_qgrad + spread_rows(part_query, chosen, 0.0)
        segment_grads.append((2 * branch_index + 1, (segment_kgrad, segment_vgrad)))
    owned, (near_scores, log_total, inner) = reduce_all(
        segment_grads, seq_index, (near_scores, log_total, inner)
    )
    near_qgrad, near_kgrad, near_vgrad = block_grads(
        near_scores, query_local, near_keys, near_values, attn_grad, log_total, inner
    )
    back_rows = shifted(
        jnp.concatenate([near_kgrad[:, :row_count], near_vgrad[:, :row_count]], 1).astype(
            jnp.bfloat16
        ),
        "seq",
        -1,
    )
    back_keys, back_values = jnp.split(back_rows.astype(jnp.float32), 2, axis=1)
    query_grad = near_qgrad
    key_grad = near_kgrad[:, row_count:] + back_keys
    value_grad = near_vgrad[:, row_count:] + back_values
    query_grad = query_grad + branch_qgrad
    for branch_entry, (own_kgrad, own_vgrad) in zip(branches, owned):
        chosen = branch_entry[1]
        key_grad = key_grad + spread_rows(own_kgrad, chosen, 0.0)
        value_grad = value_grad + spread_rows(own_vgrad, chosen, 0.0)
    flat = (row_count, head_count * HDIM)

    def to_rows(head_major):
        return head_major.astype(jnp.bfloat16).transpose(1, 0, 2).reshape(flat)

    return (to_rows(query_grad), to_rows(key_grad), to_rows(value_grad))


def solution(mesh):
    return jax.shard_map(
        per_device,
        mesh=mesh,
        in_specs=(
            P("seq", "head"),
            P("head", None),
            P("seq", "head"),
            P("seq", "head"),
            P("seq", "head"),
            P(None, "head"),
        ),
        out_specs=(P("seq", "head"), P("seq", "head"), P("seq", "head")),
        check_vma=False,
    )
```

```python
import jax
import jax.numpy as jnp
from jax import lax
from jax.sharding import PartitionSpec as P

HDIM = 128


def partner(shard, axis, stride):
    return lax.ppermute(shard, axis, [(i, i ^ 1 << stride) for i in range(lax.axis_size(axis))])


def shifted(value, axis, steps):
    count = lax.axis_size(axis)
    initial, last = (max(0, -steps), min(count, count - steps))
    return lax.ppermute(value, axis, [(source, source + steps) for source in range(initial, last)])


def pick_rows(block, chosen):
    dilation = chosen.shape[0]
    head_count = block.shape[0]
    shaped = block.reshape((head_count, block.shape[1] // dilation, dilation) + block.shape[2:])
    widened = chosen.T.reshape((head_count, 1, dilation) + (1,) * (block.ndim - 2))
    return jnp.sum(jnp.where(widened, shaped, jnp.zeros((), block.dtype)), axis=2)


def spread_rows(picked, chosen, filler):
    dilation = chosen.shape[0]
    head_count = picked.shape[0]
    widened = chosen.T.reshape((head_count, 1, dilation) + (1,) * (picked.ndim - 2))
    placed = jnp.where(widened, picked[:, :, None], jnp.asarray(filler, picked.dtype))
    return placed.reshape((head_count, picked.shape[1] * dilation) + picked.shape[2:])


def block_scores(query_rows, key_rows, key_live):
    scores = jnp.einsum(
        "hqd,hkd->hqk", query_rows, key_rows, preferred_element_type=jnp.float32
    ) * HDIM ** (-0.5)
    return jnp.where(key_live[None, None, :], scores, -jnp.inf)


def block_stats(scores):
    peak = jnp.max(scores, axis=2)
    total = jnp.sum(jnp.exp(scores - peak[:, :, None]), axis=2)
    return (peak, total)


def block_output(scores, value_rows, log_total):
    probs = jnp.exp(scores - log_total[:, :, None])
    weights = probs.astype(jnp.bfloat16)
    return jnp.einsum("hqk,hkd->hqd", weights, value_rows, preferred_element_type=jnp.float32)


def block_grads(scores, query_rows, key_rows, value_rows, out_grad, log_total, inner):
    probs = jnp.exp(scores - log_total[:, :, None])
    weights = probs.astype(jnp.bfloat16)
    flow = jnp.einsum("hqd,hkd->hqk", out_grad, value_rows, preferred_element_type=jnp.float32)
    slope = (probs * (flow - inner[:, :, None])).astype(jnp.bfloat16)
    scale = HDIM ** (-0.5)
    query_part = (
        jnp.einsum("hqk,hkd->hqd", slope, key_rows, preferred_element_type=jnp.float32) * scale
    )
    key_part = (
        jnp.einsum("hqk,hqd->hkd", slope, query_rows, preferred_element_type=jnp.float32) * scale
    )
    value_part = jnp.einsum("hqk,hqd->hkd", weights, out_grad, preferred_element_type=jnp.float32)
    return (query_part, key_part, value_part)


def exchange(arrays, bit_pos):
    sizes = [array.shape[1] for array in arrays]
    packed = jnp.concatenate(arrays, 1)
    arrived = partner(packed, "seq", bit_pos)
    cuts = [sum(sizes[: index + 1]) for index in range(len(sizes) - 1)]
    return jnp.split(arrived, cuts, axis=1)


def collect_all(groups, seq_index, tied):
    steps_total = max(steps for steps, _ in groups)
    groups = [(steps, list(parts)) for steps, parts in groups]
    for bit_pos in reversed(range(steps_total)):
        active = [index for index, (steps, _) in enumerate(groups) if steps > bit_pos]
        sending = [part for index in active for part in groups[index][1]]
        arrived = exchange(sending, bit_pos)
        if bit_pos == steps_total - 1:
            tied, _ = lax.optimization_barrier((tied, arrived[0]))
        if bit_pos == min(2, steps_total - 1):
            middle = arrived[0]
        upper = seq_index // 2**bit_pos % 2 == 1
        at = 0
        for index in active:
            parts = groups[index][1]
            merged = []
            for own_part in parts:
                far_part = arrived[at]
                at += 1
                merged.append(
                    jnp.where(
                        upper,
                        jnp.concatenate([far_part, own_part], 1),
                        jnp.concatenate([own_part, far_part], 1),
                    )
                )
            groups[index] = (groups[index][0], merged)
    return ([parts for _, parts in groups], tied, middle)


def reduce_all(groups, seq_index, tied):
    steps_total = max(steps for steps, _ in groups)
    groups = [(steps, list(parts)) for steps, parts in groups]
    for bit_pos in range(steps_total):
        active = [index for index, (steps, _) in enumerate(groups) if steps > bit_pos]
        upper = seq_index // 2**bit_pos % 2 == 1
        sending = []
        keeping = []
        for index in active:
            for whole_part in groups[index][1]:
                half_rows = whole_part.shape[1] // 2
                sending.append(
                    jnp.where(upper, whole_part[:, :half_rows], whole_part[:, half_rows:])
                )
                keeping.append(
                    jnp.where(upper, whole_part[:, half_rows:], whole_part[:, :half_rows])
                )
        arrived = exchange([part.astype(jnp.bfloat16) for part in sending], bit_pos)
        if bit_pos == 0:
            tied, _ = lax.optimization_barrier((tied, arrived[0]))
        at = 0
        for index in active:
            count = len(groups[index][1])
            groups[index] = (
                groups[index][0],
                [
                    kept + came.astype(jnp.float32)
                    for kept, came in zip(keeping[at : at + count], arrived[at : at + count])
                ],
            )
            at += count
    return ([parts for _, parts in groups], tied)


def ring_gather(block, axis):
    count = lax.axis_size(axis)
    own = lax.axis_index(axis)
    pieces = [block] + [
        lax.ppermute(block, axis, [(source, (source + step) % count) for source in range(count)])
        for step in range(1, count)
    ]
    stacked = jnp.stack(pieces)
    ordered = jnp.take(stacked, (own - jnp.arange(count)) % count, axis=0)
    return ordered.transpose(1, 0, 2).reshape(block.shape[0], count * block.shape[1])


def per_device(grad_out, out_weight, queries, keys, values, offsets):
    row_count = queries.shape[0]
    head_count = queries.shape[1] // HDIM
    branch_count = offsets.shape[0]
    view = (row_count, head_count, HDIM)

    def to_heads(flat_rows):
        return flat_rows.reshape(view).transpose(1, 0, 2)

    query_local = to_heads(queries)
    key_local = to_heads(keys)
    value_local = to_heads(values)
    seq_index = lax.axis_index("seq")
    prior_rows = shifted(jnp.concatenate([keys, values], 1), "seq", 1)
    prior_keys, prior_values = jnp.split(prior_rows, 2, axis=1)
    near_keys = jnp.concatenate([to_heads(prior_keys), key_local], 1)
    near_values = jnp.concatenate([to_heads(prior_values), value_local], 1)
    near_live = jnp.concatenate(
        [jnp.full((row_count,), seq_index > 0), jnp.ones((row_count,), jnp.bool_)]
    )
    picked_all = []
    for branch_index in range(1, branch_count + 1):
        dilation = 4**branch_index
        chosen = jnp.arange(dilation)[:, None] == offsets[branch_index - 1][None, :]
        picked_all.append(
            (
                chosen,
                pick_rows(query_local, chosen),
                pick_rows(key_local, chosen),
                pick_rows(value_local, chosen),
            )
        )
    gathered, late_grad, middle = collect_all(
        [(2 * index + 1, (entry[2], entry[3])) for index, entry in enumerate(picked_all, 1)],
        seq_index,
        grad_out,
    )
    gathered_grad, _ = lax.optimization_barrier((ring_gather(late_grad, "head"), middle))
    attn_flat = lax.dot_general(
        gathered_grad,
        out_weight,
        (((1,), (1,)), ((), ())),
        preferred_element_type=jnp.float32,
    )
    attn_grad = to_heads(attn_flat.astype(jnp.bfloat16))
    branches = []
    for branch_index in range(1, branch_count + 1):
        chosen, picked_query, picked_key, picked_value = picked_all[branch_index - 1]
        picked_grad = pick_rows(attn_grad, chosen)
        segment_keys, segment_values = gathered[branch_index - 1]
        segment_live = jnp.ones((segment_keys.shape[1],), jnp.bool_)
        seg_scores = block_scores(picked_query, segment_keys, segment_live)
        branches.append(
            (
                branch_index,
                chosen,
                picked_query,
                picked_key,
                picked_value,
                picked_grad,
                segment_keys,
                segment_values,
                seg_scores,
            )
        )
    near_scores = block_scores(query_local, near_keys, near_live)
    near_peak, near_total = block_stats(near_scores)
    peak = near_peak
    branch_stats = []
    for branch_entry in branches:
        chosen = branch_entry[1]
        seg_peak, seg_total = block_stats(branch_entry[8])
        branch_stats.append((seg_peak, seg_total))
        peak = jnp.maximum(peak, spread_rows(seg_peak, chosen, -jnp.inf))
    total = near_total * jnp.exp(near_peak - peak)
    for index_branch in range(len(branches)):
        chosen = branches[index_branch][1]
        seg_peak, seg_total = branch_stats[index_branch]
        total = total + spread_rows(
            seg_total * jnp.exp(seg_peak - pick_rows(peak, chosen)), chosen, 0.0
        )
    log_total = peak + jnp.log(total)
    output = block_output(near_scores, near_values, log_total)
    for (
        branch_index,
        chosen,
        picked_query,
        picked_key,
        picked_value,
        picked_grad,
        segment_keys,
        segment_values,
        seg_scores,
    ) in branches:
        seg_log = pick_rows(log_total, chosen)
        output = output + spread_rows(
            block_output(seg_scores, segment_values, seg_log), chosen, 0.0
        )
    inner = jnp.sum(attn_grad.astype(jnp.float32) * output, axis=2)
    segment_grads = []
    branch_qgrad = jnp.zeros(query_local.shape, jnp.float32)
    for (
        branch_index,
        chosen,
        picked_query,
        picked_key,
        picked_value,
        picked_grad,
        segment_keys,
        segment_values,
        seg_scores,
    ) in branches:
        seg_log = pick_rows(log_total, chosen)
        seg_inner = pick_rows(inner, chosen)
        part_query, segment_kgrad, segment_vgrad = block_grads(
            seg_scores, picked_query, segment_keys, segment_values, picked_grad, seg_log, seg_inner
        )
        branch_qgrad = branch_qgrad + spread_rows(part_query, chosen, 0.0)
        segment_grads.append((2 * branch_index + 1, (segment_kgrad, segment_vgrad)))
    owned, (near_scores, log_total, inner) = reduce_all(
        segment_grads, seq_index, (near_scores, log_total, inner)
    )
    near_qgrad, near_kgrad, near_vgrad = block_grads(
        near_scores, query_local, near_keys, near_values, attn_grad, log_total, inner
    )
    back_rows = shifted(
        jnp.concatenate([near_kgrad[:, :row_count], near_vgrad[:, :row_count]], 1).astype(
            jnp.bfloat16
        ),
        "seq",
        -1,
    )
    back_keys, back_values = jnp.split(back_rows.astype(jnp.float32), 2, axis=1)
    query_grad = near_qgrad
    key_grad = near_kgrad[:, row_count:] + back_keys
    value_grad = near_vgrad[:, row_count:] + back_values
    query_grad = query_grad + branch_qgrad
    for branch_entry, (own_kgrad, own_vgrad) in zip(branches, owned):
        chosen = branch_entry[1]
        key_grad = key_grad + spread_rows(own_kgrad, chosen, 0.0)
        value_grad = value_grad + spread_rows(own_vgrad, chosen, 0.0)
    flat = (row_count, head_count * HDIM)

    def to_rows(head_major):
        return head_major.astype(jnp.bfloat16).transpose(1, 0, 2).reshape(flat)

    return (to_rows(query_grad), to_rows(key_grad), to_rows(value_grad))


def solution(mesh):
    return jax.shard_map(
        per_device,
        mesh=mesh,
        in_specs=(
            P("seq", "head"),
            P("head", None),
            P("seq", "head"),
            P("seq", "head"),
            P("seq", "head"),
            P(None, "head"),
        ),
        out_specs=(P("seq", "head"), P("seq", "head"), P("seq", "head")),
        check_vma=False,
    )
```

```python
import jax
import jax.numpy as jnp
from jax import lax
from jax.sharding import PartitionSpec as P

HDIM = 128


def partner(shard, axis, stride):
    return lax.ppermute(shard, axis, [(i, i ^ 1 << stride) for i in range(lax.axis_size(axis))])


def shifted(value, axis, steps):
    count = lax.axis_size(axis)
    initial, last = (max(0, -steps), min(count, count - steps))
    return lax.ppermute(value, axis, [(source, source + steps) for source in range(initial, last)])


def pick_rows(block, chosen):
    dilation = chosen.shape[0]
    head_count = block.shape[0]
    shaped = block.reshape((head_count, block.shape[1] // dilation, dilation) + block.shape[2:])
    widened = chosen.T.reshape((head_count, 1, dilation) + (1,) * (block.ndim - 2))
    return jnp.sum(jnp.where(widened, shaped, jnp.zeros((), block.dtype)), axis=2)


def spread_rows(picked, chosen, filler):
    dilation = chosen.shape[0]
    head_count = picked.shape[0]
    widened = chosen.T.reshape((head_count, 1, dilation) + (1,) * (picked.ndim - 2))
    placed = jnp.where(widened, picked[:, :, None], jnp.asarray(filler, picked.dtype))
    return placed.reshape((head_count, picked.shape[1] * dilation) + picked.shape[2:])


def block_scores(query_rows, key_rows, key_live):
    scores = jnp.einsum(
        "hqd,hkd->hqk", query_rows, key_rows, preferred_element_type=jnp.float32
    ) * HDIM ** (-0.5)
    return jnp.where(key_live[None, None, :], scores, -jnp.inf)


def block_stats(scores):
    peak = jnp.max(scores, axis=2)
    total = jnp.sum(jnp.exp(scores - peak[:, :, None]), axis=2)
    return (peak, total)


def block_output(scores, value_rows, log_total):
    probs = jnp.exp(scores - log_total[:, :, None])
    weights = probs.astype(jnp.bfloat16)
    return jnp.einsum("hqk,hkd->hqd", weights, value_rows, preferred_element_type=jnp.float32)


def block_grads(scores, query_rows, key_rows, value_rows, out_grad, log_total, inner):
    probs = jnp.exp(scores - log_total[:, :, None])
    weights = probs.astype(jnp.bfloat16)
    flow = jnp.einsum("hqd,hkd->hqk", out_grad, value_rows, preferred_element_type=jnp.float32)
    slope = (probs * (flow - inner[:, :, None])).astype(jnp.bfloat16)
    scale = HDIM ** (-0.5)
    query_part = (
        jnp.einsum("hqk,hkd->hqd", slope, key_rows, preferred_element_type=jnp.float32) * scale
    )
    key_part = (
        jnp.einsum("hqk,hqd->hkd", slope, query_rows, preferred_element_type=jnp.float32) * scale
    )
    value_part = jnp.einsum("hqk,hqd->hkd", weights, out_grad, preferred_element_type=jnp.float32)
    return (query_part, key_part, value_part)


def exchange(arrays, bit_pos):
    sizes = [array.shape[1] for array in arrays]
    packed = jnp.concatenate(arrays, 1)
    arrived = partner(packed, "seq", bit_pos)
    cuts = [sum(sizes[: index + 1]) for index in range(len(sizes) - 1)]
    return jnp.split(arrived, cuts, axis=1)


def collect_all(groups, seq_index, tied, hooks):
    steps_total = max(steps for steps, _ in groups)
    groups = [(steps, list(parts)) for steps, parts in groups]
    for bit_pos in reversed(range(steps_total)):
        active = [index for index, (steps, _) in enumerate(groups) if steps > bit_pos]
        sending = [part for index in active for part in groups[index][1]]
        arrived = exchange(sending, bit_pos)
        if bit_pos in hooks:
            tied = hooks[bit_pos](tied, arrived[0])
        upper = seq_index // 2**bit_pos % 2 == 1
        at = 0
        for index in active:
            parts = groups[index][1]
            merged = []
            for own_part in parts:
                far_part = arrived[at]
                at += 1
                merged.append(
                    jnp.where(
                        upper,
                        jnp.concatenate([far_part, own_part], 1),
                        jnp.concatenate([own_part, far_part], 1),
                    )
                )
            groups[index] = (groups[index][0], merged)
    return ([parts for _, parts in groups], tied)


def reduce_all(groups, seq_index, tied):
    steps_total = max(steps for steps, _ in groups)
    groups = [(steps, list(parts)) for steps, parts in groups]
    for bit_pos in range(steps_total):
        active = [index for index, (steps, _) in enumerate(groups) if steps > bit_pos]
        upper = seq_index // 2**bit_pos % 2 == 1
        sending = []
        keeping = []
        for index in active:
            for whole_part in groups[index][1]:
                half_rows = whole_part.shape[1] // 2
                sending.append(
                    jnp.where(upper, whole_part[:, :half_rows], whole_part[:, half_rows:])
                )
                keeping.append(
                    jnp.where(upper, whole_part[:, half_rows:], whole_part[:, :half_rows])
                )
        arrived = exchange([part.astype(jnp.bfloat16) for part in sending], bit_pos)
        if bit_pos == 0:
            tied, _ = lax.optimization_barrier((tied, arrived[0]))
        at = 0
        for index in active:
            count = len(groups[index][1])
            groups[index] = (
                groups[index][0],
                [
                    kept + came.astype(jnp.float32)
                    for kept, came in zip(keeping[at : at + count], arrived[at : at + count])
                ],
            )
            at += count
    return ([parts for _, parts in groups], tied)


def head_step(block, axis, bit_pos):
    upper = lax.axis_index(axis) // 2**bit_pos % 2 == 1
    far = partner(block, axis, bit_pos)
    return jnp.where(upper, jnp.concatenate([far, block], 1), jnp.concatenate([block, far], 1))


def ring_gather(block, axis):
    count = lax.axis_size(axis)
    own = lax.axis_index(axis)
    pieces = [block] + [
        lax.ppermute(block, axis, [(source, (source + step) % count) for source in range(count)])
        for step in range(1, count)
    ]
    stacked = jnp.stack(pieces)
    ordered = jnp.take(stacked, (own - jnp.arange(count)) % count, axis=0)
    return ordered.transpose(1, 0, 2).reshape(block.shape[0], count * block.shape[1])


def per_device(grad_out, out_weight, queries, keys, values, offsets):
    row_count = queries.shape[0]
    head_count = queries.shape[1] // HDIM
    branch_count = offsets.shape[0]
    view = (row_count, head_count, HDIM)

    def to_heads(flat_rows):
        return flat_rows.reshape(view).transpose(1, 0, 2)

    query_local = to_heads(queries)
    key_local = to_heads(keys)
    value_local = to_heads(values)
    seq_index = lax.axis_index("seq")
    prior_rows = shifted(jnp.concatenate([keys, values], 1), "seq", 1)
    prior_keys, prior_values = jnp.split(prior_rows, 2, axis=1)
    near_keys = jnp.concatenate([to_heads(prior_keys), key_local], 1)
    near_values = jnp.concatenate([to_heads(prior_values), value_local], 1)
    near_live = jnp.concatenate(
        [jnp.full((row_count,), seq_index > 0), jnp.ones((row_count,), jnp.bool_)]
    )
    picked_all = []
    for branch_index in range(1, branch_count + 1):
        dilation = 4**branch_index
        chosen = jnp.arange(dilation)[:, None] == offsets[branch_index - 1][None, :]
        picked_all.append(
            (
                chosen,
                pick_rows(query_local, chosen),
                pick_rows(key_local, chosen),
                pick_rows(value_local, chosen),
            )
        )
    head_steps = (lax.axis_size("head") - 1).bit_length()
    steps_top = 2 * branch_count + 1

    def head_hook(step):
        def hook(block, arrived):
            block, _ = lax.optimization_barrier((block, arrived))
            return head_step(block, "head", step)

        return hook

    hooks = {steps_top - 1 - 2 * step: head_hook(step) for step in range(head_steps)}
    gathered, gathered_grad = collect_all(
        [(2 * index + 1, (entry[2], entry[3])) for index, entry in enumerate(picked_all, 1)],
        seq_index,
        grad_out,
        hooks,
    )
    gathered_grad, _ = lax.optimization_barrier((gathered_grad, gathered[-1][0]))
    attn_flat = lax.dot_general(
        gathered_grad,
        out_weight,
        (((1,), (1,)), ((), ())),
        preferred_element_type=jnp.float32,
    )
    attn_grad = to_heads(attn_flat.astype(jnp.bfloat16))
    branches = []
    for branch_index in range(1, branch_count + 1):
        chosen, picked_query, picked_key, picked_value = picked_all[branch_index - 1]
        picked_grad = pick_rows(attn_grad, chosen)
        segment_keys, segment_values = gathered[branch_index - 1]
        segment_live = jnp.ones((segment_keys.shape[1],), jnp.bool_)
        seg_scores = block_scores(picked_query, segment_keys, segment_live)
        branches.append(
            (
                branch_index,
                chosen,
                picked_query,
                picked_key,
                picked_value,
                picked_grad,
                segment_keys,
                segment_values,
                seg_scores,
            )
        )
    near_scores = block_scores(query_local, near_keys, near_live)
    near_peak, near_total = block_stats(near_scores)
    peak = near_peak
    branch_stats = []
    for branch_entry in branches:
        chosen = branch_entry[1]
        seg_peak, seg_total = block_stats(branch_entry[8])
        branch_stats.append((seg_peak, seg_total))
        peak = jnp.maximum(peak, spread_rows(seg_peak, chosen, -jnp.inf))
    total = near_total * jnp.exp(near_peak - peak)
    for index_branch in range(len(branches)):
        chosen = branches[index_branch][1]
        seg_peak, seg_total = branch_stats[index_branch]
        total = total + spread_rows(
            seg_total * jnp.exp(seg_peak - pick_rows(peak, chosen)), chosen, 0.0
        )
    log_total = peak + jnp.log(total)
    output = block_output(near_scores, near_values, log_total)
    for (
        branch_index,
        chosen,
        picked_query,
        picked_key,
        picked_value,
        picked_grad,
        segment_keys,
        segment_values,
        seg_scores,
    ) in branches:
        seg_log = pick_rows(log_total, chosen)
        output = output + spread_rows(
            block_output(seg_scores, segment_values, seg_log), chosen, 0.0
        )
    inner = jnp.sum(attn_grad.astype(jnp.float32) * output, axis=2)
    segment_grads = []
    branch_qgrad = jnp.zeros(query_local.shape, jnp.float32)
    for (
        branch_index,
        chosen,
        picked_query,
        picked_key,
        picked_value,
        picked_grad,
        segment_keys,
        segment_values,
        seg_scores,
    ) in branches:
        seg_log = pick_rows(log_total, chosen)
        seg_inner = pick_rows(inner, chosen)
        part_query, segment_kgrad, segment_vgrad = block_grads(
            seg_scores, picked_query, segment_keys, segment_values, picked_grad, seg_log, seg_inner
        )
        branch_qgrad = branch_qgrad + spread_rows(part_query, chosen, 0.0)
        segment_grads.append((2 * branch_index + 1, (segment_kgrad, segment_vgrad)))
    owned, (near_scores, log_total, inner) = reduce_all(
        segment_grads, seq_index, (near_scores, log_total, inner)
    )
    near_qgrad, near_kgrad, near_vgrad = block_grads(
        near_scores, query_local, near_keys, near_values, attn_grad, log_total, inner
    )
    back_rows = shifted(
        jnp.concatenate([near_kgrad[:, :row_count], near_vgrad[:, :row_count]], 1).astype(
            jnp.bfloat16
        ),
        "seq",
        -1,
    )
    back_keys, back_values = jnp.split(back_rows.astype(jnp.float32), 2, axis=1)
    query_grad = near_qgrad
    key_grad = near_kgrad[:, row_count:] + back_keys
    value_grad = near_vgrad[:, row_count:] + back_values
    query_grad = query_grad + branch_qgrad
    for branch_entry, (own_kgrad, own_vgrad) in zip(branches, owned):
        chosen = branch_entry[1]
        key_grad = key_grad + spread_rows(own_kgrad, chosen, 0.0)
        value_grad = value_grad + spread_rows(own_vgrad, chosen, 0.0)
    flat = (row_count, head_count * HDIM)

    def to_rows(head_major):
        return head_major.astype(jnp.bfloat16).transpose(1, 0, 2).reshape(flat)

    return (to_rows(query_grad), to_rows(key_grad), to_rows(value_grad))


def solution(mesh):
    return jax.shard_map(
        per_device,
        mesh=mesh,
        in_specs=(
            P("seq", "head"),
            P("head", None),
            P("seq", "head"),
            P("seq", "head"),
            P("seq", "head"),
            P(None, "head"),
        ),
        out_specs=(P("seq", "head"), P("seq", "head"), P("seq", "head")),
        check_vma=False,
    )
```

```python
import jax
import jax.numpy as jnp
from jax import lax
from jax.sharding import PartitionSpec as P

HDIM = 128


def partner(shard, axis, stride):
    return lax.ppermute(shard, axis, [(i, i ^ 1 << stride) for i in range(lax.axis_size(axis))])


def shifted(value, axis, steps):
    count = lax.axis_size(axis)
    initial, last = (max(0, -steps), min(count, count - steps))
    return lax.ppermute(value, axis, [(source, source + steps) for source in range(initial, last)])


def pick_rows(block, chosen):
    dilation = chosen.shape[0]
    head_count = block.shape[0]
    shaped = block.reshape((head_count, block.shape[1] // dilation, dilation) + block.shape[2:])
    widened = chosen.T.reshape((head_count, 1, dilation) + (1,) * (block.ndim - 2))
    return jnp.sum(jnp.where(widened, shaped, jnp.zeros((), block.dtype)), axis=2)


def spread_rows(picked, chosen, filler):
    dilation = chosen.shape[0]
    head_count = picked.shape[0]
    widened = chosen.T.reshape((head_count, 1, dilation) + (1,) * (picked.ndim - 2))
    placed = jnp.where(widened, picked[:, :, None], jnp.asarray(filler, picked.dtype))
    return placed.reshape((head_count, picked.shape[1] * dilation) + picked.shape[2:])


def block_scores(query_rows, key_rows, key_live):
    scores = jnp.einsum(
        "hqd,hkd->hqk", query_rows, key_rows, preferred_element_type=jnp.float32
    ) * HDIM ** (-0.5)
    return jnp.where(key_live[None, None, :], scores, -jnp.inf)


def block_stats(scores):
    peak = jnp.max(scores, axis=2)
    total = jnp.sum(jnp.exp(scores - peak[:, :, None]), axis=2)
    return (peak, total)


def block_output(scores, value_rows, log_total):
    probs = jnp.exp(scores - log_total[:, :, None])
    weights = probs.astype(jnp.bfloat16)
    return jnp.einsum("hqk,hkd->hqd", weights, value_rows, preferred_element_type=jnp.float32)


def block_grads(scores, query_rows, key_rows, value_rows, out_grad, log_total, inner):
    probs = jnp.exp(scores - log_total[:, :, None])
    weights = probs.astype(jnp.bfloat16)
    flow = jnp.einsum("hqd,hkd->hqk", out_grad, value_rows, preferred_element_type=jnp.float32)
    slope = (probs * (flow - inner[:, :, None])).astype(jnp.bfloat16)
    scale = HDIM ** (-0.5)
    query_part = (
        jnp.einsum("hqk,hkd->hqd", slope, key_rows, preferred_element_type=jnp.float32) * scale
    )
    key_part = (
        jnp.einsum("hqk,hqd->hkd", slope, query_rows, preferred_element_type=jnp.float32) * scale
    )
    value_part = jnp.einsum("hqk,hqd->hkd", weights, out_grad, preferred_element_type=jnp.float32)
    return (query_part, key_part, value_part)


def exchange(arrays, bit_pos):
    sizes = [array.shape[1] for array in arrays]
    packed = jnp.concatenate(arrays, 1)
    arrived = partner(packed, "seq", bit_pos)
    cuts = [sum(sizes[: index + 1]) for index in range(len(sizes) - 1)]
    return jnp.split(arrived, cuts, axis=1)


def collect_all(groups, seq_index, tied, hooks):
    steps_total = max(steps for steps, _ in groups)
    groups = [(steps, list(parts)) for steps, parts in groups]
    for bit_pos in reversed(range(steps_total)):
        active = [index for index, (steps, _) in enumerate(groups) if steps > bit_pos]
        sending = [part for index in active for part in groups[index][1]]
        arrived = exchange(sending, bit_pos)
        if bit_pos in hooks:
            tied = hooks[bit_pos](tied, arrived[0])
        upper = seq_index // 2**bit_pos % 2 == 1
        at = 0
        for index in active:
            parts = groups[index][1]
            merged = []
            for own_part in parts:
                far_part = arrived[at]
                at += 1
                merged.append(
                    jnp.where(
                        upper,
                        jnp.concatenate([far_part, own_part], 1),
                        jnp.concatenate([own_part, far_part], 1),
                    )
                )
            groups[index] = (groups[index][0], merged)
    return ([parts for _, parts in groups], tied)


def reduce_all(groups, seq_index, tied):
    steps_total = max(steps for steps, _ in groups)
    groups = [(steps, list(parts)) for steps, parts in groups]
    for bit_pos in range(steps_total):
        active = [index for index, (steps, _) in enumerate(groups) if steps > bit_pos]
        upper = seq_index // 2**bit_pos % 2 == 1
        sending = []
        keeping = []
        for index in active:
            for whole_part in groups[index][1]:
                half_rows = whole_part.shape[1] // 2
                sending.append(
                    jnp.where(upper, whole_part[:, :half_rows], whole_part[:, half_rows:])
                )
                keeping.append(
                    jnp.where(upper, whole_part[:, half_rows:], whole_part[:, :half_rows])
                )
        arrived = exchange([part.astype(jnp.bfloat16) for part in sending], bit_pos)
        if bit_pos == 0:
            tied, _ = lax.optimization_barrier((tied, arrived[0]))
        at = 0
        for index in active:
            count = len(groups[index][1])
            groups[index] = (
                groups[index][0],
                [
                    kept + came.astype(jnp.float32)
                    for kept, came in zip(keeping[at : at + count], arrived[at : at + count])
                ],
            )
            at += count
    return ([parts for _, parts in groups], tied)


def head_step(block, axis, bit_pos):
    upper = lax.axis_index(axis) // 2**bit_pos % 2 == 1
    far = partner(block, axis, bit_pos)
    return jnp.where(upper, jnp.concatenate([far, block], 1), jnp.concatenate([block, far], 1))


def ring_gather(block, axis):
    count = lax.axis_size(axis)
    own = lax.axis_index(axis)
    pieces = [block] + [
        lax.ppermute(block, axis, [(source, (source + step) % count) for source in range(count)])
        for step in range(1, count)
    ]
    stacked = jnp.stack(pieces)
    ordered = jnp.take(stacked, (own - jnp.arange(count)) % count, axis=0)
    return ordered.transpose(1, 0, 2).reshape(block.shape[0], count * block.shape[1])


def per_device(grad_out, out_weight, queries, keys, values, offsets):
    row_count = queries.shape[0]
    head_count = queries.shape[1] // HDIM
    branch_count = offsets.shape[0]
    view = (row_count, head_count, HDIM)

    def to_heads(flat_rows):
        return flat_rows.reshape(view).transpose(1, 0, 2)

    query_local = to_heads(queries)
    key_local = to_heads(keys)
    value_local = to_heads(values)
    seq_index = lax.axis_index("seq")
    prior_rows = shifted(jnp.concatenate([keys, values], 1), "seq", 1)
    prior_keys, prior_values = jnp.split(prior_rows, 2, axis=1)
    near_keys = jnp.concatenate([to_heads(prior_keys), key_local], 1)
    near_values = jnp.concatenate([to_heads(prior_values), value_local], 1)
    near_live = jnp.concatenate(
        [jnp.full((row_count,), seq_index > 0), jnp.ones((row_count,), jnp.bool_)]
    )
    picked_all = []
    for branch_index in range(1, branch_count + 1):
        dilation = 4**branch_index
        chosen = jnp.arange(dilation)[:, None] == offsets[branch_index - 1][None, :]
        picked_all.append(
            (
                chosen,
                pick_rows(query_local, chosen),
                pick_rows(key_local, chosen),
                pick_rows(value_local, chosen),
            )
        )
    head_steps = (lax.axis_size("head") - 1).bit_length()
    steps_top = 2 * branch_count + 1

    def head_hook(step):
        def hook(block, arrived):
            block, _ = lax.optimization_barrier((block, arrived))
            return head_step(block, "head", step)

        return hook

    hooks = {
        steps_top - 1 - 2 * step: head_hook(head_steps - 1 - step) for step in range(head_steps)
    }
    gathered, gathered_grad = collect_all(
        [(2 * index + 1, (entry[2], entry[3])) for index, entry in enumerate(picked_all, 1)],
        seq_index,
        grad_out,
        hooks,
    )
    gathered_grad, _ = lax.optimization_barrier((gathered_grad, gathered[-1][0]))
    block_cols = grad_out.shape[1]
    gathered_grad = jnp.concatenate(
        [
            gathered_grad[:, place * block_cols : (place + 1) * block_cols]
            for place in [
                int(format(head, f"0{head_steps}b")[::-1], 2)
                for head in range(lax.axis_size("head"))
            ]
        ],
        1,
    )
    attn_flat = lax.dot_general(
        gathered_grad,
        out_weight,
        (((1,), (1,)), ((), ())),
        preferred_element_type=jnp.float32,
    )
    attn_grad = to_heads(attn_flat.astype(jnp.bfloat16))
    branches = []
    for branch_index in range(1, branch_count + 1):
        chosen, picked_query, picked_key, picked_value = picked_all[branch_index - 1]
        picked_grad = pick_rows(attn_grad, chosen)
        segment_keys, segment_values = gathered[branch_index - 1]
        segment_live = jnp.ones((segment_keys.shape[1],), jnp.bool_)
        seg_scores = block_scores(picked_query, segment_keys, segment_live)
        branches.append(
            (
                branch_index,
                chosen,
                picked_query,
                picked_key,
                picked_value,
                picked_grad,
                segment_keys,
                segment_values,
                seg_scores,
            )
        )
    near_scores = block_scores(query_local, near_keys, near_live)
    near_peak, near_total = block_stats(near_scores)
    peak = near_peak
    branch_stats = []
    for branch_entry in branches:
        chosen = branch_entry[1]
        seg_peak, seg_total = block_stats(branch_entry[8])
        branch_stats.append((seg_peak, seg_total))
        peak = jnp.maximum(peak, spread_rows(seg_peak, chosen, -jnp.inf))
    total = near_total * jnp.exp(near_peak - peak)
    for index_branch in range(len(branches)):
        chosen = branches[index_branch][1]
        seg_peak, seg_total = branch_stats[index_branch]
        total = total + spread_rows(
            seg_total * jnp.exp(seg_peak - pick_rows(peak, chosen)), chosen, 0.0
        )
    log_total = peak + jnp.log(total)
    output = block_output(near_scores, near_values, log_total)
    for (
        branch_index,
        chosen,
        picked_query,
        picked_key,
        picked_value,
        picked_grad,
        segment_keys,
        segment_values,
        seg_scores,
    ) in branches:
        seg_log = pick_rows(log_total, chosen)
        output = output + spread_rows(
            block_output(seg_scores, segment_values, seg_log), chosen, 0.0
        )
    inner = jnp.sum(attn_grad.astype(jnp.float32) * output, axis=2)
    segment_grads = []
    branch_qgrad = jnp.zeros(query_local.shape, jnp.float32)
    for (
        branch_index,
        chosen,
        picked_query,
        picked_key,
        picked_value,
        picked_grad,
        segment_keys,
        segment_values,
        seg_scores,
    ) in branches:
        seg_log = pick_rows(log_total, chosen)
        seg_inner = pick_rows(inner, chosen)
        part_query, segment_kgrad, segment_vgrad = block_grads(
            seg_scores, picked_query, segment_keys, segment_values, picked_grad, seg_log, seg_inner
        )
        branch_qgrad = branch_qgrad + spread_rows(part_query, chosen, 0.0)
        segment_grads.append((2 * branch_index + 1, (segment_kgrad, segment_vgrad)))
    owned, (near_scores, log_total, inner) = reduce_all(
        segment_grads, seq_index, (near_scores, log_total, inner)
    )
    near_qgrad, near_kgrad, near_vgrad = block_grads(
        near_scores, query_local, near_keys, near_values, attn_grad, log_total, inner
    )
    back_rows = shifted(
        jnp.concatenate([near_kgrad[:, :row_count], near_vgrad[:, :row_count]], 1).astype(
            jnp.bfloat16
        ),
        "seq",
        -1,
    )
    back_keys, back_values = jnp.split(back_rows.astype(jnp.float32), 2, axis=1)
    query_grad = near_qgrad
    key_grad = near_kgrad[:, row_count:] + back_keys
    value_grad = near_vgrad[:, row_count:] + back_values
    query_grad = query_grad + branch_qgrad
    for branch_entry, (own_kgrad, own_vgrad) in zip(branches, owned):
        chosen = branch_entry[1]
        key_grad = key_grad + spread_rows(own_kgrad, chosen, 0.0)
        value_grad = value_grad + spread_rows(own_vgrad, chosen, 0.0)
    flat = (row_count, head_count * HDIM)

    def to_rows(head_major):
        return head_major.astype(jnp.bfloat16).transpose(1, 0, 2).reshape(flat)

    return (to_rows(query_grad), to_rows(key_grad), to_rows(value_grad))


def solution(mesh):
    return jax.shard_map(
        per_device,
        mesh=mesh,
        in_specs=(
            P("seq", "head"),
            P("head", None),
            P("seq", "head"),
            P("seq", "head"),
            P("seq", "head"),
            P(None, "head"),
        ),
        out_specs=(P("seq", "head"), P("seq", "head"), P("seq", "head")),
        check_vma=False,
    )
```

```python
import jax
import jax.numpy as jnp
from jax import lax
from jax.sharding import PartitionSpec as P

HDIM = 128


def partner(shard, axis, stride):
    return lax.ppermute(shard, axis, [(i, i ^ 1 << stride) for i in range(lax.axis_size(axis))])


def shifted(value, axis, steps):
    count = lax.axis_size(axis)
    initial, last = (max(0, -steps), min(count, count - steps))
    return lax.ppermute(value, axis, [(source, source + steps) for source in range(initial, last)])


def pick_rows(block, chosen):
    dilation = chosen.shape[0]
    head_count = block.shape[0]
    shaped = block.reshape((head_count, block.shape[1] // dilation, dilation) + block.shape[2:])
    widened = chosen.T.reshape((head_count, 1, dilation) + (1,) * (block.ndim - 2))
    return jnp.sum(jnp.where(widened, shaped, jnp.zeros((), block.dtype)), axis=2)


def spread_rows(picked, chosen, filler):
    dilation = chosen.shape[0]
    head_count = picked.shape[0]
    widened = chosen.T.reshape((head_count, 1, dilation) + (1,) * (picked.ndim - 2))
    placed = jnp.where(widened, picked[:, :, None], jnp.asarray(filler, picked.dtype))
    return placed.reshape((head_count, picked.shape[1] * dilation) + picked.shape[2:])


def block_scores(query_rows, key_rows, key_live):
    scores = jnp.einsum(
        "hqd,hkd->hqk", query_rows, key_rows, preferred_element_type=jnp.float32
    ) * HDIM ** (-0.5)
    return jnp.where(key_live[None, None, :], scores, -jnp.inf)


def block_stats(scores):
    peak = jnp.max(scores, axis=2)
    total = jnp.sum(jnp.exp(scores - peak[:, :, None]), axis=2)
    return (peak, total)


def block_output(scores, value_rows, log_total):
    probs = jnp.exp(scores - log_total[:, :, None])
    weights = probs.astype(jnp.bfloat16)
    return jnp.einsum("hqk,hkd->hqd", weights, value_rows, preferred_element_type=jnp.float32)


def block_grads(scores, query_rows, key_rows, value_rows, out_grad, log_total, inner):
    probs = jnp.exp(scores - log_total[:, :, None])
    weights = probs.astype(jnp.bfloat16)
    flow = jnp.einsum("hqd,hkd->hqk", out_grad, value_rows, preferred_element_type=jnp.float32)
    slope = (probs * (flow - inner[:, :, None])).astype(jnp.bfloat16)
    scale = HDIM ** (-0.5)
    query_part = (
        jnp.einsum("hqk,hkd->hqd", slope, key_rows, preferred_element_type=jnp.float32) * scale
    )
    key_part = (
        jnp.einsum("hqk,hqd->hkd", slope, query_rows, preferred_element_type=jnp.float32) * scale
    )
    value_part = jnp.einsum("hqk,hqd->hkd", weights, out_grad, preferred_element_type=jnp.float32)
    return (query_part, key_part, value_part)


def exchange(arrays, bit_pos):
    sizes = [array.shape[1] for array in arrays]
    packed = jnp.concatenate(arrays, 1)
    arrived = partner(packed, "seq", bit_pos)
    cuts = [sum(sizes[: index + 1]) for index in range(len(sizes) - 1)]
    return jnp.split(arrived, cuts, axis=1)


def collect_all(groups, seq_index, tied, hooks):
    steps_total = max(steps for steps, _ in groups)
    groups = [(steps, list(parts)) for steps, parts in groups]
    for bit_pos in reversed(range(steps_total)):
        active = [index for index, (steps, _) in enumerate(groups) if steps > bit_pos]
        sending = [part for index in active for part in groups[index][1]]
        arrived = exchange(sending, bit_pos)
        if bit_pos in hooks:
            tied = hooks[bit_pos](tied, arrived[0])
        upper = seq_index // 2**bit_pos % 2 == 1
        at = 0
        for index in active:
            parts = groups[index][1]
            merged = []
            for own_part in parts:
                far_part = arrived[at]
                at += 1
                merged.append(
                    jnp.where(
                        upper,
                        jnp.concatenate([far_part, own_part], 1),
                        jnp.concatenate([own_part, far_part], 1),
                    )
                )
            groups[index] = (groups[index][0], merged)
    return ([parts for _, parts in groups], tied)


def reduce_all(groups, seq_index, tied):
    steps_total = max(steps for steps, _ in groups)
    groups = [(steps, list(parts)) for steps, parts in groups]
    for bit_pos in range(steps_total):
        active = [index for index, (steps, _) in enumerate(groups) if steps > bit_pos]
        upper = seq_index // 2**bit_pos % 2 == 1
        sending = []
        keeping = []
        for index in active:
            for whole_part in groups[index][1]:
                half_rows = whole_part.shape[1] // 2
                sending.append(
                    jnp.where(upper, whole_part[:, :half_rows], whole_part[:, half_rows:])
                )
                keeping.append(
                    jnp.where(upper, whole_part[:, half_rows:], whole_part[:, :half_rows])
                )
        arrived = exchange([part.astype(jnp.bfloat16) for part in sending], bit_pos)
        if bit_pos == 0:
            tied, _ = lax.optimization_barrier((tied, arrived[0]))
        at = 0
        for index in active:
            count = len(groups[index][1])
            groups[index] = (
                groups[index][0],
                [
                    kept + came.astype(jnp.float32)
                    for kept, came in zip(keeping[at : at + count], arrived[at : at + count])
                ],
            )
            at += count
    return ([parts for _, parts in groups], tied)


def head_step(block, axis, bit_pos):
    upper = lax.axis_index(axis) // 2**bit_pos % 2 == 1
    far = partner(block, axis, bit_pos)
    return jnp.where(upper, jnp.concatenate([far, block], 1), jnp.concatenate([block, far], 1))


def ring_gather(block, axis):
    count = lax.axis_size(axis)
    own = lax.axis_index(axis)
    pieces = [block] + [
        lax.ppermute(block, axis, [(source, (source + step) % count) for source in range(count)])
        for step in range(1, count)
    ]
    stacked = jnp.stack(pieces)
    ordered = jnp.take(stacked, (own - jnp.arange(count)) % count, axis=0)
    return ordered.transpose(1, 0, 2).reshape(block.shape[0], count * block.shape[1])


def per_device(grad_out, out_weight, queries, keys, values, offsets):
    row_count = queries.shape[0]
    head_count = queries.shape[1] // HDIM
    branch_count = offsets.shape[0]
    view = (row_count, head_count, HDIM)

    def to_heads(flat_rows):
        return flat_rows.reshape(view).transpose(1, 0, 2)

    query_local = to_heads(queries)
    key_local = to_heads(keys)
    value_local = to_heads(values)
    seq_index = lax.axis_index("seq")
    prior_rows = shifted(jnp.concatenate([keys, values], 1), "seq", 1)
    prior_keys, prior_values = jnp.split(prior_rows, 2, axis=1)
    near_keys = jnp.concatenate([to_heads(prior_keys), key_local], 1)
    near_values = jnp.concatenate([to_heads(prior_values), value_local], 1)
    near_live = jnp.concatenate(
        [jnp.full((row_count,), seq_index > 0), jnp.ones((row_count,), jnp.bool_)]
    )
    picked_all = []
    for branch_index in range(1, branch_count + 1):
        dilation = 4**branch_index
        chosen = jnp.arange(dilation)[:, None] == offsets[branch_index - 1][None, :]
        picked_all.append(
            (
                chosen,
                pick_rows(query_local, chosen),
                pick_rows(key_local, chosen),
                pick_rows(value_local, chosen),
            )
        )
    head_steps = (lax.axis_size("head") - 1).bit_length()
    steps_top = 2 * branch_count + 1

    def head_hook(step):
        def hook(block, arrived):
            block, _ = lax.optimization_barrier((block, arrived))
            return head_step(block, "head", step)

        return hook

    hooks = {
        steps_top - 1 - step: head_hook(head_steps - 1 - step) for step in range(head_steps)
    }
    gathered, gathered_grad = collect_all(
        [(2 * index + 1, (entry[2], entry[3])) for index, entry in enumerate(picked_all, 1)],
        seq_index,
        grad_out,
        hooks,
    )
    gathered_grad, _ = lax.optimization_barrier((gathered_grad, gathered[-1][0]))
    block_cols = grad_out.shape[1]
    gathered_grad = jnp.concatenate(
        [
            gathered_grad[:, place * block_cols : (place + 1) * block_cols]
            for place in [
                int(format(head, f"0{head_steps}b")[::-1], 2)
                for head in range(lax.axis_size("head"))
            ]
        ],
        1,
    )
    attn_flat = lax.dot_general(
        gathered_grad,
        out_weight,
        (((1,), (1,)), ((), ())),
        preferred_element_type=jnp.float32,
    )
    attn_grad = to_heads(attn_flat.astype(jnp.bfloat16))
    branches = []
    for branch_index in range(1, branch_count + 1):
        chosen, picked_query, picked_key, picked_value = picked_all[branch_index - 1]
        picked_grad = pick_rows(attn_grad, chosen)
        segment_keys, segment_values = gathered[branch_index - 1]
        segment_live = jnp.ones((segment_keys.shape[1],), jnp.bool_)
        seg_scores = block_scores(picked_query, segment_keys, segment_live)
        branches.append(
            (
                branch_index,
                chosen,
                picked_query,
                picked_key,
                picked_value,
                picked_grad,
                segment_keys,
                segment_values,
                seg_scores,
            )
        )
    near_scores = block_scores(query_local, near_keys, near_live)
    near_peak, near_total = block_stats(near_scores)
    peak = near_peak
    branch_stats = []
    for branch_entry in branches:
        chosen = branch_entry[1]
        seg_peak, seg_total = block_stats(branch_entry[8])
        branch_stats.append((seg_peak, seg_total))
        peak = jnp.maximum(peak, spread_rows(seg_peak, chosen, -jnp.inf))
    total = near_total * jnp.exp(near_peak - peak)
    for index_branch in range(len(branches)):
        chosen = branches[index_branch][1]
        seg_peak, seg_total = branch_stats[index_branch]
        total = total + spread_rows(
            seg_total * jnp.exp(seg_peak - pick_rows(peak, chosen)), chosen, 0.0
        )
    log_total = peak + jnp.log(total)
    output = block_output(near_scores, near_values, log_total)
    for (
        branch_index,
        chosen,
        picked_query,
        picked_key,
        picked_value,
        picked_grad,
        segment_keys,
        segment_values,
        seg_scores,
    ) in branches:
        seg_log = pick_rows(log_total, chosen)
        output = output + spread_rows(
            block_output(seg_scores, segment_values, seg_log), chosen, 0.0
        )
    inner = jnp.sum(attn_grad.astype(jnp.float32) * output, axis=2)
    segment_grads = []
    branch_qgrad = jnp.zeros(query_local.shape, jnp.float32)
    for (
        branch_index,
        chosen,
        picked_query,
        picked_key,
        picked_value,
        picked_grad,
        segment_keys,
        segment_values,
        seg_scores,
    ) in branches:
        seg_log = pick_rows(log_total, chosen)
        seg_inner = pick_rows(inner, chosen)
        part_query, segment_kgrad, segment_vgrad = block_grads(
            seg_scores, picked_query, segment_keys, segment_values, picked_grad, seg_log, seg_inner
        )
        branch_qgrad = branch_qgrad + spread_rows(part_query, chosen, 0.0)
        segment_grads.append((2 * branch_index + 1, (segment_kgrad, segment_vgrad)))
    owned, (near_scores, log_total, inner) = reduce_all(
        segment_grads, seq_index, (near_scores, log_total, inner)
    )
    near_qgrad, near_kgrad, near_vgrad = block_grads(
        near_scores, query_local, near_keys, near_values, attn_grad, log_total, inner
    )
    back_rows = shifted(
        jnp.concatenate([near_kgrad[:, :row_count], near_vgrad[:, :row_count]], 1).astype(
            jnp.bfloat16
        ),
        "seq",
        -1,
    )
    back_keys, back_values = jnp.split(back_rows.astype(jnp.float32), 2, axis=1)
    query_grad = near_qgrad
    key_grad = near_kgrad[:, row_count:] + back_keys
    value_grad = near_vgrad[:, row_count:] + back_values
    query_grad = query_grad + branch_qgrad
    for branch_entry, (own_kgrad, own_vgrad) in zip(branches, owned):
        chosen = branch_entry[1]
        key_grad = key_grad + spread_rows(own_kgrad, chosen, 0.0)
        value_grad = value_grad + spread_rows(own_vgrad, chosen, 0.0)
    flat = (row_count, head_count * HDIM)

    def to_rows(head_major):
        return head_major.astype(jnp.bfloat16).transpose(1, 0, 2).reshape(flat)

    return (to_rows(query_grad), to_rows(key_grad), to_rows(value_grad))


def solution(mesh):
    return jax.shard_map(
        per_device,
        mesh=mesh,
        in_specs=(
            P("seq", "head"),
            P("head", None),
            P("seq", "head"),
            P("seq", "head"),
            P("seq", "head"),
            P(None, "head"),
        ),
        out_specs=(P("seq", "head"), P("seq", "head"), P("seq", "head")),
        check_vma=False,
    )
```

```python
import jax
import jax.numpy as jnp
from jax import lax
from jax.sharding import PartitionSpec as P

HDIM = 128


def partner(shard, axis, stride):
    return lax.ppermute(shard, axis, [(i, i ^ 1 << stride) for i in range(lax.axis_size(axis))])


def shifted(value, axis, steps):
    count = lax.axis_size(axis)
    initial, last = (max(0, -steps), min(count, count - steps))
    return lax.ppermute(value, axis, [(source, source + steps) for source in range(initial, last)])


def pick_rows(block, chosen):
    dilation = chosen.shape[0]
    head_count = block.shape[0]
    shaped = block.reshape((head_count, block.shape[1] // dilation, dilation) + block.shape[2:])
    widened = chosen.T.reshape((head_count, 1, dilation) + (1,) * (block.ndim - 2))
    return jnp.sum(jnp.where(widened, shaped, jnp.zeros((), block.dtype)), axis=2)


def pick_flat(flat_rows, chosen):
    dilation, head_count = chosen.shape
    shaped = flat_rows.reshape(flat_rows.shape[0] // dilation, dilation, flat_rows.shape[1])
    widened = jnp.repeat(chosen, HDIM, axis=1)[None]
    picked = jnp.sum(jnp.where(widened, shaped, jnp.zeros((), flat_rows.dtype)), axis=1)
    return picked.reshape(picked.shape[0], head_count, HDIM).transpose(1, 0, 2)


def spread_rows(picked, chosen, filler):
    dilation = chosen.shape[0]
    head_count = picked.shape[0]
    widened = chosen.T.reshape((head_count, 1, dilation) + (1,) * (picked.ndim - 2))
    placed = jnp.where(widened, picked[:, :, None], jnp.asarray(filler, picked.dtype))
    return placed.reshape((head_count, picked.shape[1] * dilation) + picked.shape[2:])


def block_scores(query_rows, key_rows, key_live):
    scores = jnp.einsum(
        "hqd,hkd->hqk", query_rows, key_rows, preferred_element_type=jnp.float32
    ) * HDIM ** (-0.5)
    return jnp.where(key_live[None, None, :], scores, -jnp.inf)


def block_stats(scores):
    peak = jnp.max(scores, axis=2)
    total = jnp.sum(jnp.exp(scores - peak[:, :, None]), axis=2)
    return (peak, total)


def block_output(scores, value_rows, log_total):
    probs = jnp.exp(scores - log_total[:, :, None])
    weights = probs.astype(jnp.bfloat16)
    return jnp.einsum("hqk,hkd->hqd", weights, value_rows, preferred_element_type=jnp.float32)


def block_grads(scores, query_rows, key_rows, value_rows, out_grad, log_total, inner):
    probs = jnp.exp(scores - log_total[:, :, None])
    weights = probs.astype(jnp.bfloat16)
    flow = jnp.einsum("hqd,hkd->hqk", out_grad, value_rows, preferred_element_type=jnp.float32)
    slope = (probs * (flow - inner[:, :, None])).astype(jnp.bfloat16)
    scale = HDIM ** (-0.5)
    query_part = (
        jnp.einsum("hqk,hkd->hqd", slope, key_rows, preferred_element_type=jnp.float32) * scale
    )
    key_part = (
        jnp.einsum("hqk,hqd->hkd", slope, query_rows, preferred_element_type=jnp.float32) * scale
    )
    value_part = jnp.einsum("hqk,hqd->hkd", weights, out_grad, preferred_element_type=jnp.float32)
    return (query_part, key_part, value_part)


def exchange(arrays, bit_pos):
    sizes = [array.shape[1] for array in arrays]
    packed = jnp.concatenate(arrays, 1)
    arrived = partner(packed, "seq", bit_pos)
    cuts = [sum(sizes[: index + 1]) for index in range(len(sizes) - 1)]
    return jnp.split(arrived, cuts, axis=1)


def collect_all(groups, seq_index, tied, hooks):
    steps_total = max(steps for steps, _ in groups)
    groups = [(steps, list(parts)) for steps, parts in groups]
    for bit_pos in reversed(range(steps_total)):
        active = [index for index, (steps, _) in enumerate(groups) if steps > bit_pos]
        sending = [part for index in active for part in groups[index][1]]
        arrived = exchange(sending, bit_pos)
        if bit_pos in hooks:
            tied = hooks[bit_pos](tied, arrived[0])
        upper = seq_index // 2**bit_pos % 2 == 1
        at = 0
        for index in active:
            parts = groups[index][1]
            merged = []
            for own_part in parts:
                far_part = arrived[at]
                at += 1
                merged.append(
                    jnp.where(
                        upper,
                        jnp.concatenate([far_part, own_part], 1),
                        jnp.concatenate([own_part, far_part], 1),
                    )
                )
            groups[index] = (groups[index][0], merged)
    return ([parts for _, parts in groups], tied)


def reduce_all(groups, seq_index, tied):
    steps_total = max(steps for steps, _ in groups)
    groups = [(steps, list(parts)) for steps, parts in groups]
    for bit_pos in range(steps_total):
        active = [index for index, (steps, _) in enumerate(groups) if steps > bit_pos]
        upper = seq_index // 2**bit_pos % 2 == 1
        sending = []
        keeping = []
        for index in active:
            for whole_part in groups[index][1]:
                half_rows = whole_part.shape[1] // 2
                sending.append(
                    jnp.where(upper, whole_part[:, :half_rows], whole_part[:, half_rows:])
                )
                keeping.append(
                    jnp.where(upper, whole_part[:, half_rows:], whole_part[:, :half_rows])
                )
        arrived = exchange([part.astype(jnp.bfloat16) for part in sending], bit_pos)
        if bit_pos == 0:
            tied, _ = lax.optimization_barrier((tied, arrived[0]))
        at = 0
        for index in active:
            count = len(groups[index][1])
            groups[index] = (
                groups[index][0],
                [
                    kept + came.astype(jnp.float32)
                    for kept, came in zip(keeping[at : at + count], arrived[at : at + count])
                ],
            )
            at += count
    return ([parts for _, parts in groups], tied)


def head_step(block, axis, bit_pos):
    upper = lax.axis_index(axis) // 2**bit_pos % 2 == 1
    far = partner(block, axis, bit_pos)
    return jnp.where(upper, jnp.concatenate([far, block], 1), jnp.concatenate([block, far], 1))


def ring_gather(block, axis):
    count = lax.axis_size(axis)
    own = lax.axis_index(axis)
    pieces = [block] + [
        lax.ppermute(block, axis, [(source, (source + step) % count) for source in range(count)])
        for step in range(1, count)
    ]
    stacked = jnp.stack(pieces)
    ordered = jnp.take(stacked, (own - jnp.arange(count)) % count, axis=0)
    return ordered.transpose(1, 0, 2).reshape(block.shape[0], count * block.shape[1])


def per_device(grad_out, out_weight, queries, keys, values, offsets):
    row_count = queries.shape[0]
    head_count = queries.shape[1] // HDIM
    branch_count = offsets.shape[0]
    view = (row_count, head_count, HDIM)

    def to_heads(flat_rows):
        return flat_rows.reshape(view).transpose(1, 0, 2)

    query_local = to_heads(queries)
    key_local = to_heads(keys)
    value_local = to_heads(values)
    seq_index = lax.axis_index("seq")
    prior_rows = shifted(jnp.concatenate([keys, values], 1), "seq", 1)
    prior_keys, prior_values = jnp.split(prior_rows, 2, axis=1)
    near_keys = jnp.concatenate([to_heads(prior_keys), key_local], 1)
    near_values = jnp.concatenate([to_heads(prior_values), value_local], 1)
    near_live = jnp.concatenate(
        [jnp.full((row_count,), seq_index > 0), jnp.ones((row_count,), jnp.bool_)]
    )
    picked_all = []
    for branch_index in range(1, branch_count + 1):
        dilation = 4**branch_index
        chosen = jnp.arange(dilation)[:, None] == offsets[branch_index - 1][None, :]
        picked_all.append(
            (
                chosen,
                pick_rows(query_local, chosen),
                pick_flat(keys, chosen),
                pick_flat(values, chosen),
            )
        )
    head_steps = (lax.axis_size("head") - 1).bit_length()
    steps_top = 2 * branch_count + 1

    def head_hook(step):
        def hook(block, arrived):
            block, _ = lax.optimization_barrier((block, arrived))
            return head_step(block, "head", step)

        return hook

    hooks = {
        steps_top - 1 - 2 * step: head_hook(head_steps - 1 - step) for step in range(head_steps)
    }
    gathered, gathered_grad = collect_all(
        [(2 * index + 1, (entry[2], entry[3])) for index, entry in enumerate(picked_all, 1)],
        seq_index,
        grad_out,
        hooks,
    )
    gathered_grad, _ = lax.optimization_barrier((gathered_grad, gathered[-1][0]))
    block_cols = grad_out.shape[1]
    gathered_grad = jnp.concatenate(
        [
            gathered_grad[:, place * block_cols : (place + 1) * block_cols]
            for place in [
                int(format(head, f"0{head_steps}b")[::-1], 2)
                for head in range(lax.axis_size("head"))
            ]
        ],
        1,
    )
    attn_flat = lax.dot_general(
        gathered_grad,
        out_weight,
        (((1,), (1,)), ((), ())),
        preferred_element_type=jnp.float32,
    )
    attn_grad = to_heads(attn_flat.astype(jnp.bfloat16))
    branches = []
    for branch_index in range(1, branch_count + 1):
        chosen, picked_query, picked_key, picked_value = picked_all[branch_index - 1]
        picked_grad = pick_rows(attn_grad, chosen)
        segment_keys, segment_values = gathered[branch_index - 1]
        segment_live = jnp.ones((segment_keys.shape[1],), jnp.bool_)
        seg_scores = block_scores(picked_query, segment_keys, segment_live)
        branches.append(
            (
                branch_index,
                chosen,
                picked_query,
                picked_key,
                picked_value,
                picked_grad,
                segment_keys,
                segment_values,
                seg_scores,
            )
        )
    near_scores = block_scores(query_local, near_keys, near_live)
    near_peak, near_total = block_stats(near_scores)
    peak = near_peak
    branch_stats = []
    for branch_entry in branches:
        chosen = branch_entry[1]
        seg_peak, seg_total = block_stats(branch_entry[8])
        branch_stats.append((seg_peak, seg_total))
        peak = jnp.maximum(peak, spread_rows(seg_peak, chosen, -jnp.inf))
    total = near_total * jnp.exp(near_peak - peak)
    for index_branch in range(len(branches)):
        chosen = branches[index_branch][1]
        seg_peak, seg_total = branch_stats[index_branch]
        total = total + spread_rows(
            seg_total * jnp.exp(seg_peak - pick_rows(peak, chosen)), chosen, 0.0
        )
    log_total = peak + jnp.log(total)
    output = block_output(near_scores, near_values, log_total)
    for (
        branch_index,
        chosen,
        picked_query,
        picked_key,
        picked_value,
        picked_grad,
        segment_keys,
        segment_values,
        seg_scores,
    ) in branches:
        seg_log = pick_rows(log_total, chosen)
        output = output + spread_rows(
            block_output(seg_scores, segment_values, seg_log), chosen, 0.0
        )
    inner = jnp.sum(attn_grad.astype(jnp.float32) * output, axis=2)
    segment_grads = []
    branch_qgrad = jnp.zeros(query_local.shape, jnp.float32)
    for (
        branch_index,
        chosen,
        picked_query,
        picked_key,
        picked_value,
        picked_grad,
        segment_keys,
        segment_values,
        seg_scores,
    ) in branches:
        seg_log = pick_rows(log_total, chosen)
        seg_inner = pick_rows(inner, chosen)
        part_query, segment_kgrad, segment_vgrad = block_grads(
            seg_scores, picked_query, segment_keys, segment_values, picked_grad, seg_log, seg_inner
        )
        branch_qgrad = branch_qgrad + spread_rows(part_query, chosen, 0.0)
        segment_grads.append((2 * branch_index + 1, (segment_kgrad, segment_vgrad)))
    owned, (near_scores, log_total, inner) = reduce_all(
        segment_grads, seq_index, (near_scores, log_total, inner)
    )
    near_qgrad, near_kgrad, near_vgrad = block_grads(
        near_scores, query_local, near_keys, near_values, attn_grad, log_total, inner
    )
    back_rows = shifted(
        jnp.concatenate([near_kgrad[:, :row_count], near_vgrad[:, :row_count]], 1).astype(
            jnp.bfloat16
        ),
        "seq",
        -1,
    )
    back_keys, back_values = jnp.split(back_rows.astype(jnp.float32), 2, axis=1)
    query_grad = near_qgrad
    key_grad = near_kgrad[:, row_count:] + back_keys
    value_grad = near_vgrad[:, row_count:] + back_values
    query_grad = query_grad + branch_qgrad
    for branch_entry, (own_kgrad, own_vgrad) in zip(branches, owned):
        chosen = branch_entry[1]
        key_grad = key_grad + spread_rows(own_kgrad, chosen, 0.0)
        value_grad = value_grad + spread_rows(own_vgrad, chosen, 0.0)
    flat = (row_count, head_count * HDIM)

    def to_rows(head_major):
        return head_major.astype(jnp.bfloat16).transpose(1, 0, 2).reshape(flat)

    return (to_rows(query_grad), to_rows(key_grad), to_rows(value_grad))


def solution(mesh):
    return jax.shard_map(
        per_device,
        mesh=mesh,
        in_specs=(
            P("seq", "head"),
            P("head", None),
            P("seq", "head"),
            P("seq", "head"),
            P("seq", "head"),
            P(None, "head"),
        ),
        out_specs=(P("seq", "head"), P("seq", "head"), P("seq", "head")),
        check_vma=False,
    )
```

```python
import jax
import jax.numpy as jnp
from jax import lax
from jax.sharding import PartitionSpec as P

HDIM = 128


def partner(shard, axis, stride):
    return lax.ppermute(shard, axis, [(i, i ^ 1 << stride) for i in range(lax.axis_size(axis))])


def shifted(value, axis, steps):
    count = lax.axis_size(axis)
    initial, last = (max(0, -steps), min(count, count - steps))
    return lax.ppermute(value, axis, [(source, source + steps) for source in range(initial, last)])


def pick_rows(block, chosen):
    dilation = chosen.shape[0]
    head_count = block.shape[0]
    shaped = block.reshape((head_count, block.shape[1] // dilation, dilation) + block.shape[2:])
    widened = chosen.T.reshape((head_count, 1, dilation) + (1,) * (block.ndim - 2))
    return jnp.sum(jnp.where(widened, shaped, jnp.zeros((), block.dtype)), axis=2)


def spread_rows(picked, chosen, filler):
    dilation = chosen.shape[0]
    head_count = picked.shape[0]
    widened = chosen.T.reshape((head_count, 1, dilation) + (1,) * (picked.ndim - 2))
    placed = jnp.where(widened, picked[:, :, None], jnp.asarray(filler, picked.dtype))
    return placed.reshape((head_count, picked.shape[1] * dilation) + picked.shape[2:])


def block_scores(query_rows, key_rows, key_live):
    scores = jnp.einsum(
        "hqd,hkd->hqk", query_rows, key_rows, preferred_element_type=jnp.float32
    ) * HDIM ** (-0.5)
    return jnp.where(key_live[None, None, :], scores, -jnp.inf)


def block_stats(scores):
    peak = jnp.max(scores, axis=2)
    total = jnp.sum(jnp.exp(scores - peak[:, :, None]), axis=2)
    return (peak, total)


def block_output(scores, value_rows, log_total):
    probs = jnp.exp(scores - log_total[:, :, None])
    weights = probs.astype(jnp.bfloat16)
    return jnp.einsum("hqk,hkd->hqd", weights, value_rows, preferred_element_type=jnp.float32)


def block_grads(scores, query_rows, key_rows, value_rows, out_grad, log_total, inner):
    probs = jnp.exp(scores - log_total[:, :, None])
    weights = probs.astype(jnp.bfloat16)
    flow = jnp.einsum("hqd,hkd->hqk", out_grad, value_rows, preferred_element_type=jnp.float32)
    slope = (probs * (flow - inner[:, :, None])).astype(jnp.bfloat16)
    scale = HDIM ** (-0.5)
    query_part = (
        jnp.einsum("hqk,hkd->hqd", slope, key_rows, preferred_element_type=jnp.float32) * scale
    )
    key_part = (
        jnp.einsum("hqk,hqd->hkd", slope, query_rows, preferred_element_type=jnp.float32) * scale
    )
    value_part = jnp.einsum("hqk,hqd->hkd", weights, out_grad, preferred_element_type=jnp.float32)
    return (query_part, key_part, value_part)


def exchange(arrays, bit_pos):
    sizes = [array.shape[1] for array in arrays]
    packed = jnp.concatenate(arrays, 1)
    arrived = partner(packed, "seq", bit_pos)
    cuts = [sum(sizes[: index + 1]) for index in range(len(sizes) - 1)]
    return jnp.split(arrived, cuts, axis=1)


def collect_all(groups, seq_index, tied, hooks):
    steps_total = max(steps for steps, _ in groups)
    groups = [(steps, list(parts)) for steps, parts in groups]
    for bit_pos in reversed(range(steps_total)):
        active = [index for index, (steps, _) in enumerate(groups) if steps > bit_pos]
        sending = [part for index in active for part in groups[index][1]]
        arrived = exchange(sending, bit_pos)
        if bit_pos in hooks:
            tied = hooks[bit_pos](tied, arrived[0])
        upper = seq_index // 2**bit_pos % 2 == 1
        at = 0
        for index in active:
            parts = groups[index][1]
            merged = []
            for own_part in parts:
                far_part = arrived[at]
                at += 1
                merged.append(
                    jnp.where(
                        upper,
                        jnp.concatenate([far_part, own_part], 1),
                        jnp.concatenate([own_part, far_part], 1),
                    )
                )
            groups[index] = (groups[index][0], merged)
    return ([parts for _, parts in groups], tied)


def reduce_all(groups, seq_index, tied, make_last):
    steps_total = max(steps for steps, _ in groups)
    groups = [(steps, list(parts)) for steps, parts in groups]
    for bit_pos in range(steps_total):
        active = [index for index, (steps, _) in enumerate(groups) if steps > bit_pos]
        upper = seq_index // 2**bit_pos % 2 == 1
        sending = []
        keeping = []
        for index in active:
            for whole_part in groups[index][1]:
                half_rows = whole_part.shape[1] // 2
                sending.append(
                    jnp.where(upper, whole_part[:, :half_rows], whole_part[:, half_rows:])
                )
                keeping.append(
                    jnp.where(upper, whole_part[:, half_rows:], whole_part[:, :half_rows])
                )
        if bit_pos == steps_total - 1:
            sending, tied = lax.optimization_barrier((sending, make_last(tied)))
        arrived = exchange([part.astype(jnp.bfloat16) for part in sending], bit_pos)
        if bit_pos == 0:
            tied, _ = lax.optimization_barrier((tied, arrived[0]))
        at = 0
        for index in active:
            count = len(groups[index][1])
            groups[index] = (
                groups[index][0],
                [
                    kept + came.astype(jnp.float32)
                    for kept, came in zip(keeping[at : at + count], arrived[at : at + count])
                ],
            )
            at += count
    return ([parts for _, parts in groups], tied)


def head_step(block, axis, bit_pos):
    upper = lax.axis_index(axis) // 2**bit_pos % 2 == 1
    far = partner(block, axis, bit_pos)
    return jnp.where(upper, jnp.concatenate([far, block], 1), jnp.concatenate([block, far], 1))


def ring_gather(block, axis):
    count = lax.axis_size(axis)
    own = lax.axis_index(axis)
    pieces = [block] + [
        lax.ppermute(block, axis, [(source, (source + step) % count) for source in range(count)])
        for step in range(1, count)
    ]
    stacked = jnp.stack(pieces)
    ordered = jnp.take(stacked, (own - jnp.arange(count)) % count, axis=0)
    return ordered.transpose(1, 0, 2).reshape(block.shape[0], count * block.shape[1])


def per_device(grad_out, out_weight, queries, keys, values, offsets):
    row_count = queries.shape[0]
    head_count = queries.shape[1] // HDIM
    branch_count = offsets.shape[0]
    view = (row_count, head_count, HDIM)

    def to_heads(flat_rows):
        return flat_rows.reshape(view).transpose(1, 0, 2)

    query_local = to_heads(queries)
    key_local = to_heads(keys)
    value_local = to_heads(values)
    seq_index = lax.axis_index("seq")
    prior_rows = shifted(jnp.concatenate([keys, values], 1), "seq", 1)
    prior_keys, prior_values = jnp.split(prior_rows, 2, axis=1)
    near_keys = jnp.concatenate([to_heads(prior_keys), key_local], 1)
    near_values = jnp.concatenate([to_heads(prior_values), value_local], 1)
    near_live = jnp.concatenate(
        [jnp.full((row_count,), seq_index > 0), jnp.ones((row_count,), jnp.bool_)]
    )
    picked_all = []
    for branch_index in range(1, branch_count + 1):
        dilation = 4**branch_index
        chosen = jnp.arange(dilation)[:, None] == offsets[branch_index - 1][None, :]
        picked_all.append(
            (
                chosen,
                pick_rows(query_local, chosen),
                pick_rows(key_local, chosen),
                pick_rows(value_local, chosen),
            )
        )
    head_steps = (lax.axis_size("head") - 1).bit_length()
    steps_top = 2 * branch_count + 1

    def head_hook(step):
        def hook(block, arrived):
            block, _ = lax.optimization_barrier((block, arrived))
            return head_step(block, "head", step)

        return hook

    hooks = {
        steps_top - 1 - 2 * step: head_hook(head_steps - 1 - step) for step in range(head_steps)
    }
    gathered, gathered_grad = collect_all(
        [(2 * index + 1, (entry[2], entry[3])) for index, entry in enumerate(picked_all, 1)],
        seq_index,
        grad_out,
        hooks,
    )
    gathered_grad, _ = lax.optimization_barrier((gathered_grad, gathered[-1][0]))
    block_cols = grad_out.shape[1]
    gathered_grad = jnp.concatenate(
        [
            gathered_grad[:, place * block_cols : (place + 1) * block_cols]
            for place in [
                int(format(head, f"0{head_steps}b")[::-1], 2)
                for head in range(lax.axis_size("head"))
            ]
        ],
        1,
    )
    attn_flat = lax.dot_general(
        gathered_grad,
        out_weight,
        (((1,), (1,)), ((), ())),
        preferred_element_type=jnp.float32,
    )
    attn_grad = to_heads(attn_flat.astype(jnp.bfloat16))
    branches = []
    for branch_index in range(1, branch_count + 1):
        chosen, picked_query, picked_key, picked_value = picked_all[branch_index - 1]
        picked_grad = pick_rows(attn_grad, chosen)
        segment_keys, segment_values = gathered[branch_index - 1]
        segment_live = jnp.ones((segment_keys.shape[1],), jnp.bool_)
        seg_scores = block_scores(picked_query, segment_keys, segment_live)
        branches.append(
            (
                branch_index,
                chosen,
                picked_query,
                picked_key,
                picked_value,
                picked_grad,
                segment_keys,
                segment_values,
                seg_scores,
            )
        )
    near_scores = block_scores(query_local, near_keys, near_live)
    near_peak, near_total = block_stats(near_scores)
    peak = near_peak
    branch_stats = []
    for branch_entry in branches:
        chosen = branch_entry[1]
        seg_peak, seg_total = block_stats(branch_entry[8])
        branch_stats.append((seg_peak, seg_total))
        peak = jnp.maximum(peak, spread_rows(seg_peak, chosen, -jnp.inf))
    total = near_total * jnp.exp(near_peak - peak)
    for index_branch in range(len(branches)):
        chosen = branches[index_branch][1]
        seg_peak, seg_total = branch_stats[index_branch]
        total = total + spread_rows(
            seg_total * jnp.exp(seg_peak - pick_rows(peak, chosen)), chosen, 0.0
        )
    log_total = peak + jnp.log(total)
    output = block_output(near_scores, near_values, log_total)
    for (
        branch_index,
        chosen,
        picked_query,
        picked_key,
        picked_value,
        picked_grad,
        segment_keys,
        segment_values,
        seg_scores,
    ) in branches:
        seg_log = pick_rows(log_total, chosen)
        output = output + spread_rows(
            block_output(seg_scores, segment_values, seg_log), chosen, 0.0
        )
    inner = jnp.sum(attn_grad.astype(jnp.float32) * output, axis=2)
    segment_grads = []
    branch_qgrad = jnp.zeros(query_local.shape, jnp.float32)
    for (
        branch_index,
        chosen,
        picked_query,
        picked_key,
        picked_value,
        picked_grad,
        segment_keys,
        segment_values,
        seg_scores,
    ) in branches:
        seg_log = pick_rows(log_total, chosen)
        seg_inner = pick_rows(inner, chosen)
        part_query, segment_kgrad, segment_vgrad = block_grads(
            seg_scores, picked_query, segment_keys, segment_values, picked_grad, seg_log, seg_inner
        )
        branch_qgrad = branch_qgrad + spread_rows(part_query, chosen, 0.0)
        segment_grads.append((2 * branch_index + 1, (segment_kgrad, segment_vgrad)))
    flat = (row_count, head_count * HDIM)

    def to_rows(head_major):
        return head_major.astype(jnp.bfloat16).transpose(1, 0, 2).reshape(flat)

    def near_backward(near_inputs):
        near_grads = block_grads(
            near_inputs[0], query_local, near_keys, near_values, attn_grad, *near_inputs[1:]
        )
        return near_grads + (to_rows(near_grads[0] + branch_qgrad),)

    owned, (near_qgrad, near_kgrad, near_vgrad, query_rows) = reduce_all(
        segment_grads, seq_index, (near_scores, log_total, inner), near_backward
    )
    back_rows = shifted(
        jnp.concatenate([near_kgrad[:, :row_count], near_vgrad[:, :row_count]], 1).astype(
            jnp.bfloat16
        ),
        "seq",
        -1,
    )
    back_keys, back_values = jnp.split(back_rows.astype(jnp.float32), 2, axis=1)
    key_grad = near_kgrad[:, row_count:] + back_keys
    value_grad = near_vgrad[:, row_count:] + back_values
    for branch_entry, (own_kgrad, own_vgrad) in zip(branches, owned):
        chosen = branch_entry[1]
        key_grad = key_grad + spread_rows(own_kgrad, chosen, 0.0)
        value_grad = value_grad + spread_rows(own_vgrad, chosen, 0.0)
    return (query_rows, to_rows(key_grad), to_rows(value_grad))


def solution(mesh):
    return jax.shard_map(
        per_device,
        mesh=mesh,
        in_specs=(
            P("seq", "head"),
            P("head", None),
            P("seq", "head"),
            P("seq", "head"),
            P("seq", "head"),
            P(None, "head"),
        ),
        out_specs=(P("seq", "head"), P("seq", "head"), P("seq", "head")),
        check_vma=False,
    )
```
